256 devices in a mesh: seq: 64 (over x, y_hi, z), head: 4 (over y_lo, core).
Axes of the slice: x: 4, y: 4 (y_hi: 2, y_lo: 2; y = y_hi * 2 + y_lo), z: 8, core: 2. Of those that a mesh axis runs over, the one named last changes fastest.
Arguments:
- tokens: bfloat16 [16384, 5376], P('seq'), may hold values from -6 to 6
- q_weight: bfloat16 [5376, 2048], P('seq', 'head')
- k_weight: bfloat16 [5376, 1024], P('seq', 'head')
- v_weight: bfloat16 [5376, 1024], P('seq', 'head'), may hold values from -0.078125 to 0.078125
- q_gain: float32 [128], replicated, may hold values from 0.5 to 6
- k_gain: float32 [128], replicated, may hold values from 0.5 to 6
- windows: int32 [16], P('head'), may hold values from 512 to 1024, as said below
- token_weight: float32 [16384], P('seq'), may hold values from 0.3 to 6
- loss_mask: int32 [16384], P('seq'), may hold values from 0 to 1, as said below
- grad_attn: bfloat16 [16384, 2048], P('seq', 'head'), may hold values from -6 to 6
Outputs:
- attn: bfloat16 [16384, 2048], P('seq', 'head')
- grad_tokens: bfloat16 [16384, 5376], P('seq', 'head')
The draws below stay inside these ranges and needn't reach their ends.
Inputs may be any that keep to these rules, and one draw needn't show every extreme that they name: `windows`: some head has a window of exactly 1024 keys and some head exactly 512. `loss_mask`: the first token always counts.
All inputs are finite; a program needn't handle non-finite values.
Results may differ from the reference program's by a relative error of at most 0.038.
The reference program's roundings to bfloat16 on the way count: a program that leaves them out, or rounds other values in their place, can miss the bound.
Values may be sent and summed in bfloat16 or wider, within the bound.
No kernel may reach another device: no remote copies, remote signals or barrier semaphores. Data moves between devices by JAX's collectives and lax.ppermute only.
A program may use at most 128 MiB of HBM per device.

```python
import jax
import jax.numpy as jnp
from jax import lax

D = 5376
HQ = 16
KV = 8
HD = 128
QPRE = 168
WINDOW = 1024
TOK_DEV = 256
TOKENS = 16384


def query_matrix(key):
    base_key = jax.random.fold_in(key, 11)
    matrix = jax.random.normal(base_key, (D, HQ * HD), jnp.float32) * D ** (-0.5)
    return matrix


def draw_q_weight(key, part):
    return query_matrix(key).astype(jnp.bfloat16)


def draw_k_weight(key, part):
    noise = jax.random.normal(jax.random.fold_in(key, 12), (D, KV * HD), jnp.float32) * D ** (-0.5)
    result = noise
    return result.astype(jnp.bfloat16)


def gain_draw(key, salt):
    sub_key = jax.random.fold_in(key, salt)
    result = jax.random.uniform(sub_key, (HD,), jnp.float32, 0.5, 1.6)
    return result


def draw_q_gain(key, part):
    return gain_draw(key, 13)


def draw_k_gain(key, part):
    return gain_draw(key, 14)


def draw_token_weight(key, part):
    sub_key = jax.random.fold_in(key, 15)
    ramp = 1.0 + 2.0 * jnp.arange(TOKENS, dtype=jnp.float32) / TOKENS
    spread = jax.random.uniform(sub_key, (TOKENS,), jnp.float32, 0.5, 1.5)
    return spread * ramp


def draw_loss_mask(key, part):
    sub_key = jax.random.fold_in(key, 16)
    positions = jnp.arange(TOKENS, dtype=jnp.int32)
    thresholds = 300 + 600 * positions // TOKENS
    draws = jax.random.randint(sub_key, (TOKENS,), 0, 1000, dtype=jnp.int32)
    result = (draws < thresholds).astype(jnp.int32)
    return result.at[0].set(1)


def draw_windows(key, part):
    sub_key = jax.random.fold_in(key, 17)
    key_one, key_two, key_three = jax.random.split(sub_key, 3)
    lengths = jax.random.randint(key_one, (HQ,), WINDOW // 2, WINDOW + 1, dtype=jnp.int32)
    longest = jax.random.randint(key_two, (), 0, HQ, dtype=jnp.int32)
    shortest = (longest + 1 + jax.random.randint(key_three, (), 0, HQ - 1, dtype=jnp.int32)) % HQ
    return lengths.at[longest].set(WINDOW).at[shortest].set(WINDOW // 2)


def level_of(key, extent, cuts, smallest, top_value):
    def one(position, parts):
        heights = jax.random.uniform(jax.random.fold_in(jax.random.fold_in(key, 6), position), (parts,), jnp.float32, smallest / len(cuts), top_value / len(cuts))
        return jnp.repeat(jnp.exp(heights), extent[position] // parts).reshape((-1,) + (1,) * (len(extent) - position - 1))

    factor_of = one(*cuts[0])
    for cut in cuts[1:]:
        factor_of = factor_of * one(*cut)
    return factor_of


def normal_values(key, shape, scale, limit, cuts=(), held_as=jnp.bfloat16):
    values = scale * jax.random.normal(key, shape, jnp.float32)
    if cuts:
        values = values * level_of(key, shape, cuts, -0.22, 0.18)
    return jnp.clip(values, -limit, limit).astype(held_as)


def setup_inputs(seed: int = 0) -> dict:
    keys = jax.random.split(jax.random.key(seed), 11)
    return {
        "tokens": normal_values(keys[0], (TOKENS, D), 1.0, 6.0, ((0, 64),)),
        "q_weight": draw_q_weight(jax.random.fold_in(keys[10], 71), 0),
        "k_weight": draw_k_weight(jax.random.fold_in(keys[10], 71), 0),
        "v_weight": normal_values(keys[3], (D, KV * HD), D ** -0.5, 0.078125, ((0, 64), (1, 4))),
        "q_gain": draw_q_gain(jax.random.fold_in(keys[10], 71), 0),
        "k_gain": draw_k_gain(jax.random.fold_in(keys[10], 71), 0),
        "windows": draw_windows(jax.random.fold_in(keys[10], 71), 0),
        "token_weight": draw_token_weight(jax.random.fold_in(keys[10], 71), 0),
        "loss_mask": draw_loss_mask(jax.random.fold_in(keys[10], 71), 0),
        "grad_attn": normal_values(keys[9], (TOKENS, HQ * HD), 1.0, 6.0, ((0, 64), (1, 4))),
    }


norm_eps = 1e-06

def rotate_table(positions, head_width):
    half_width = head_width // 2
    frequency = 10000.0 ** (-(jnp.arange(half_width, dtype=jnp.float32) * 2.0) / head_width)
    angles = positions.astype(jnp.float32)[:, None] * frequency[None, :]
    return (jnp.cos(angles)[:, None, :], jnp.sin(angles)[:, None, :])

def norm_rotate(linear, gain_vec, cosine, sine_table):
    mean_square = lax.optimization_barrier(jnp.mean(linear * linear, axis=-1, keepdims=True))
    normed = linear * lax.rsqrt(mean_square + norm_eps) * gain_vec
    half_width = linear.shape[-1] // 2
    first_half = normed[..., :half_width]
    second_half = normed[..., half_width:]
    return jnp.concatenate([first_half * cosine - second_half * sine_table, second_half * cosine + first_half * sine_table], axis=-1)

def block_grad(queries, key_rows, value_rows, cotangent, query_pos, key_pos, windows, score_scale):
    tok_rows, q_heads, head_width = queries.shape
    kv_heads = key_rows.shape[1]
    group_size = q_heads // kv_heads
    query_grp = queries.reshape(tok_rows, kv_heads, group_size, head_width).astype(jnp.float32)
    cotan_grp = cotangent.reshape(tok_rows, kv_heads, group_size, head_width).astype(jnp.float32)
    key_float = key_rows.astype(jnp.float32)
    value_float = value_rows.astype(jnp.float32)
    scores = score_scale * jnp.einsum('tgjd,sgd->gjts', query_grp, key_float)
    distance = query_pos[:, None] - key_pos[None, :]
    reach = windows.reshape(kv_heads, group_size)[:, :, None, None]
    allowed = (distance[None, None] >= 0) & (distance[None, None] < reach) & (key_pos >= 0)[None, None, None, :]
    masked = jnp.where(allowed, scores, jnp.float32(-1e+30))
    row_peak = lax.optimization_barrier(jnp.max(masked, axis=-1, keepdims=True))
    row_total = lax.optimization_barrier(jnp.sum(jnp.where(allowed, jnp.exp(masked - row_peak), jnp.float32(0.0)), axis=-1, keepdims=True))
    logsum = row_peak + jnp.log(row_total)
    probability = jnp.where(allowed, jnp.exp(masked - logsum), jnp.float32(0.0))
    probs_b = probability.astype(jnp.bfloat16)
    attended = jnp.einsum('gjts,sgd->tgjd', probs_b.astype(jnp.float32), value_float).astype(jnp.bfloat16)
    row_delta = lax.optimization_barrier(jnp.sum(cotan_grp * attended.astype(jnp.float32), axis=-1))
    dprobs = jnp.einsum('tgjd,sgd->gjts', cotan_grp, value_float)
    dscore = (probability * (dprobs - jnp.transpose(row_delta, (1, 2, 0))[..., None])).astype(jnp.bfloat16)
    dscore_f = dscore.astype(jnp.float32)
    dquery = score_scale * jnp.einsum('gjts,sgd->tgjd', dscore_f, key_float)
    key_grads = score_scale * jnp.einsum('gjts,tgjd->sgd', dscore_f, query_grp)
    dvalues = jnp.einsum('gjts,tgjd->sgd', probs_b.astype(jnp.float32), cotan_grp)
    return (attended.reshape(tok_rows, q_heads * head_width), dquery.reshape(tok_rows, q_heads, head_width), key_grads, dvalues)

def reference(tokens, q_weight, k_weight, v_weight, q_gain, k_gain, windows, token_weight, loss_mask, grad_attn):
    score_scale = QPRE ** (-0.5)
    lead_rows = WINDOW // TOK_DEV * TOK_DEV
    key_span = lead_rows + TOK_DEV
    q_linear = jnp.dot(tokens, q_weight, preferred_element_type=jnp.float32).reshape(TOKENS, HQ, HD)
    k_linear = jnp.dot(tokens, k_weight, preferred_element_type=jnp.float32).reshape(TOKENS, KV, HD)
    values = jnp.dot(tokens, v_weight, preferred_element_type=jnp.float32).astype(jnp.bfloat16).reshape(TOKENS, KV, HD)
    positions = jnp.arange(TOKENS, dtype=jnp.int32)
    cosine, sine_table = rotate_table(positions, HD)
    q_rot = norm_rotate(q_linear, q_gain, cosine, sine_table).astype(jnp.bfloat16)
    k_rot = norm_rotate(k_linear, k_gain, cosine, sine_table).astype(jnp.bfloat16)
    kept_weight = token_weight * loss_mask.astype(jnp.float32)
    normalizer = jnp.sum(kept_weight)
    factor = kept_weight * (TOKENS / normalizer)
    cotangent = (grad_attn.astype(jnp.float32) * factor[:, None]).astype(jnp.bfloat16).reshape(TOKENS, HQ, HD)
    key_pad = jnp.concatenate([jnp.zeros((lead_rows, KV, HD), jnp.bfloat16), k_rot], axis=0)
    value_pad = jnp.concatenate([jnp.zeros((lead_rows, KV, HD), jnp.bfloat16), values], axis=0)

    def block_step(carried, block_idx):
        key_acc, value_acc = carried
        first_row = (block_idx * TOK_DEV).astype(jnp.int32)
        queries = lax.dynamic_slice_in_dim(q_rot, first_row, TOK_DEV, 0)
        cotan_rows = lax.dynamic_slice_in_dim(cotangent, first_row, TOK_DEV, 0)
        key_rows = lax.dynamic_slice_in_dim(key_pad, first_row, key_span, 0)
        value_rows = lax.dynamic_slice_in_dim(value_pad, first_row, key_span, 0)
        query_pos = first_row + jnp.arange(TOK_DEV, dtype=jnp.int32)
        key_pos = first_row - lead_rows + jnp.arange(key_span, dtype=jnp.int32)
        attended, dquery, key_grads, dvalues = block_grad(queries, key_rows, value_rows, cotan_rows, query_pos, key_pos, windows, score_scale)
        key_acc = lax.dynamic_update_slice_in_dim(key_acc, lax.dynamic_slice_in_dim(key_acc, first_row, key_span, 0) + key_grads, first_row, 0)
        value_acc = lax.dynamic_update_slice_in_dim(value_acc, lax.dynamic_slice_in_dim(value_acc, first_row, key_span, 0) + dvalues, first_row, 0)
        return ((key_acc, value_acc), (attended, dquery))
    zero_rows = jnp.zeros((lead_rows + TOKENS, KV, HD), jnp.float32)
    (key_acc, value_acc), (attended, dquery) = lax.scan(block_step, (zero_rows, zero_rows), jnp.arange(TOKENS // TOK_DEV, dtype=jnp.int32))
    attn = attended.reshape(TOKENS, HQ * HD)
    dquery = dquery.reshape(TOKENS, HQ, HD)
    _, back_query = jax.vjp(lambda linear_in: norm_rotate(linear_in, q_gain, cosine, sine_table), q_linear)
    _, back_key = jax.vjp(lambda linear_in: norm_rotate(linear_in, k_gain, cosine, sine_table), k_linear)
    dq_lin = back_query(dquery)[0].astype(jnp.bfloat16).reshape(TOKENS, HQ * HD)
    dk_lin = back_key(key_acc[lead_rows:])[0].astype(jnp.bfloat16).reshape(TOKENS, KV * HD)
    dv_lin = value_acc[lead_rows:].astype(jnp.bfloat16).reshape(TOKENS, KV * HD)
    contract = (((1,), (1,)), ((), ()))
    grad_sum = lax.dot_general(dq_lin, q_weight, contract, preferred_element_type=jnp.float32)
    grad_sum = grad_sum + lax.dot_general(dk_lin, k_weight, contract, preferred_element_type=jnp.float32)
    grad_sum = grad_sum + lax.dot_general(dv_lin, v_weight, contract, preferred_element_type=jnp.float32)
    return (attn, grad_sum.astype(jnp.bfloat16))
```

```python
import jax
import jax.numpy as jnp
from jax import lax
from jax.sharding import PartitionSpec as P

QPRE = 168
WINDOW = 1024


norm_eps = 1e-06


def passed_along(block, axis, distance):
    devices = range(lax.axis_size(axis))
    route = [(i - distance, i) for i in devices if i - distance in devices]
    return lax.ppermute(block, axis, route)


def rotate_table(positions, head_width):
    half_width = head_width // 2
    frequency = 10000.0 ** (-(jnp.arange(half_width, dtype=jnp.float32) * 2.0) / head_width)
    angles = positions.astype(jnp.float32)[:, None] * frequency[None, :]
    return (jnp.cos(angles)[:, None, :], jnp.sin(angles)[:, None, :])


def norm_rotate(linear, gain_vec, cosine, sine_table):
    mean_square = jnp.mean(linear * linear, axis=-1, keepdims=True)
    normed = linear * lax.rsqrt(mean_square + norm_eps) * gain_vec
    half_width = linear.shape[-1] // 2
    first_half = normed[..., :half_width]
    second_half = normed[..., half_width:]
    return jnp.concatenate(
        [
            first_half * cosine - second_half * sine_table,
            second_half * cosine + first_half * sine_table,
        ],
        axis=-1,
    )


def block_grad(queries, key_rows, value_rows, cotangent, query_pos, key_pos, windows, score_scale):
    tok_rows, q_heads, head_width = queries.shape
    kv_heads = key_rows.shape[1]
    group_size = q_heads // kv_heads
    query_grp = queries.reshape(tok_rows, kv_heads, group_size, head_width)
    cotan_grp = cotangent.reshape(tok_rows, kv_heads, group_size, head_width)
    scores = score_scale * jnp.einsum(
        "tgjd,sgd->gjts", query_grp, key_rows, preferred_element_type=jnp.float32
    )
    distance = query_pos[:, None] - key_pos[None, :]
    reach = windows.reshape(kv_heads, group_size)[:, :, None, None]
    allowed = (
        (distance[None, None] >= 0)
        & (distance[None, None] < reach)
        & (key_pos >= 0)[None, None, None, :]
    )
    masked = jnp.where(allowed, scores, jnp.float32(-1e30))
    row_peak = jnp.max(masked, axis=-1, keepdims=True)
    row_total = jnp.sum(
        jnp.where(allowed, jnp.exp(masked - row_peak), jnp.float32(0.0)), axis=-1, keepdims=True
    )
    logsum = row_peak + jnp.log(row_total)
    probability = jnp.where(allowed, jnp.exp(masked - logsum), jnp.float32(0.0))
    probs_b = probability.astype(jnp.bfloat16)
    attended = jnp.einsum(
        "gjts,sgd->tgjd", probs_b, value_rows, preferred_element_type=jnp.float32
    ).astype(jnp.bfloat16)
    row_delta = jnp.sum(cotan_grp.astype(jnp.float32) * attended.astype(jnp.float32), axis=-1)
    dprobs = jnp.einsum("tgjd,sgd->gjts", cotan_grp, value_rows, preferred_element_type=jnp.float32)
    dscore = (probability * (dprobs - jnp.transpose(row_delta, (1, 2, 0))[..., None])).astype(
        jnp.bfloat16
    )
    dquery = score_scale * jnp.einsum(
        "gjts,sgd->tgjd", dscore, key_rows, preferred_element_type=jnp.float32
    )
    key_grads = score_scale * jnp.einsum(
        "gjts,tgjd->sgd", dscore, query_grp, preferred_element_type=jnp.float32
    )
    dvalues = jnp.einsum("gjts,tgjd->sgd", probs_b, cotan_grp, preferred_element_type=jnp.float32)
    return (
        attended.reshape(tok_rows, q_heads * head_width),
        dquery.reshape(tok_rows, q_heads, head_width),
        key_grads,
        dvalues,
    )


def body(
    tokens,
    q_weight,
    k_weight,
    v_weight,
    q_gain,
    k_gain,
    windows,
    token_weight,
    loss_mask,
    grad_attn,
):
    tok_rows = tokens.shape[0]
    head_width = q_gain.shape[0]
    q_heads = q_weight.shape[1] // head_width
    kv_heads = k_weight.shape[1] // head_width
    pred_count = WINDOW // tok_rows
    key_span = (pred_count + 1) * tok_rows
    score_scale = QPRE ** (-0.5)
    first_row = lax.axis_index("seq") * tok_rows
    positions = first_row + jnp.arange(tok_rows, dtype=jnp.int32)
    key_pos = first_row - pred_count * tok_rows + jnp.arange(key_span, dtype=jnp.int32)
    kept_weight = token_weight * loss_mask.astype(jnp.float32)
    normalizer = lax.psum(jnp.sum(kept_weight), "seq")
    factor = kept_weight * (tok_rows * lax.axis_size("seq") / normalizer)
    cotangent = (
        (grad_attn.astype(jnp.float32) * factor[:, None])
        .astype(jnp.bfloat16)
        .reshape(tok_rows, q_heads, head_width)
    )
    contract = (((1,), (1,)), ((), ()))
    q_cols = q_weight.shape[1]
    k_cols = k_weight.shape[1]
    joined_rows = lax.all_gather(
        jnp.concatenate([q_weight, k_weight, v_weight], axis=1), "seq", axis=0, tiled=True
    )
    all_linear = jnp.dot(tokens, joined_rows, preferred_element_type=jnp.float32)
    q_linear = all_linear[:, :q_cols]
    k_linear = all_linear[:, q_cols : q_cols + k_cols]
    v_linear = all_linear[:, q_cols + k_cols :]
    q_linear = q_linear.reshape(tok_rows, q_heads, head_width)
    k_linear = k_linear.reshape(tok_rows, kv_heads, head_width)
    values = v_linear.astype(jnp.bfloat16)
    cosine, sine_table = rotate_table(positions, head_width)
    q_rot = norm_rotate(q_linear, q_gain, cosine, sine_table).astype(jnp.bfloat16)
    k_rot = norm_rotate(k_linear, k_gain, cosine, sine_table).astype(jnp.bfloat16)
    stacked = jnp.stack([k_rot.reshape(tok_rows, kv_heads * head_width), values])
    received = []
    for offset in range(1, pred_count + 1):
        received.append(passed_along(stacked, "seq", offset))
    extended = jnp.concatenate(received[::-1] + [stacked], axis=1)
    key_rows = extended[0].reshape(key_span, kv_heads, head_width)
    value_rows = extended[1].reshape(key_span, kv_heads, head_width)
    attended, dquery, key_grads, dvalues = block_grad(
        q_rot, key_rows, value_rows, cotangent, positions, key_pos, windows, score_scale
    )
    stacked_grads = jnp.stack(
        [
            key_grads.reshape(key_span, kv_heads * head_width),
            dvalues.reshape(key_span, kv_heads * head_width),
        ]
    )
    local_grads = stacked_grads[:, pred_count * tok_rows :]
    for offset in range(1, pred_count + 1):
        local_grads = local_grads + passed_along(
            stacked_grads[
                :, (pred_count - offset) * tok_rows : (pred_count - offset + 1) * tok_rows
            ].astype(jnp.bfloat16),
            "seq",
            -offset,
        ).astype(jnp.float32)
    key_total = local_grads[0].reshape(tok_rows, kv_heads, head_width)
    _, back_query = jax.vjp(
        lambda linear_in: norm_rotate(linear_in, q_gain, cosine, sine_table), q_linear
    )
    _, back_key = jax.vjp(
        lambda linear_in: norm_rotate(linear_in, k_gain, cosine, sine_table), k_linear
    )
    dq_lin = back_query(dquery)[0].astype(jnp.bfloat16).reshape(tok_rows, q_heads * head_width)
    dk_lin = back_key(key_total)[0].astype(jnp.bfloat16).reshape(tok_rows, kv_heads * head_width)
    dv_lin = local_grads[1].astype(jnp.bfloat16)
    joined_grad = jnp.concatenate([dq_lin, dk_lin, dv_lin], axis=1)
    partial_grad = lax.dot_general(
        joined_grad,
        joined_rows,
        contract,
        preferred_element_type=jnp.float32,
    )
    grad_tokens = lax.psum_scatter(
        partial_grad.astype(jnp.bfloat16), "head", scatter_dimension=1, tiled=True
    )
    return (attended, grad_tokens)


def solution(mesh):
    in_specs = (
        P("seq", None),
        P("seq", "head"),
        P("seq", "head"),
        P("seq", "head"),
        P(),
        P(),
        P("head"),
        P("seq"),
        P("seq"),
        P("seq", "head"),
    )
    out_specs = (P("seq", "head"), P("seq", "head"))
    return jax.shard_map(body, mesh=mesh, in_specs=in_specs, out_specs=out_specs, check_vma=False)
```

```python
import jax
import jax.numpy as jnp
from jax import lax
from jax.sharding import PartitionSpec as P

QPRE = 168
WINDOW = 1024


norm_eps = 1e-06


def passed_along(block, axis, distance):
    devices = range(lax.axis_size(axis))
    route = [(i - distance, i) for i in devices if i - distance in devices]
    return lax.ppermute(block, axis, route)


def butterfly_sum(value, axis):
    size = lax.axis_size(axis)
    step = 1
    while step < size:
        value = value + lax.ppermute(value, axis, [(i, i ^ step) for i in range(size)])
        step *= 2
    return value


def head_scatter_sum(partial, axis):
    rows, width = partial.shape
    index = lax.axis_index(axis)
    parts = partial.reshape(rows, 2, 2, width // 4)
    low_bit = index % 2
    high_bit = index // 2
    kept = lax.dynamic_index_in_dim(parts, low_bit, axis=2, keepdims=False)
    sent = lax.dynamic_index_in_dim(parts, 1 - low_bit, axis=2, keepdims=False)
    got = lax.ppermute(sent.astype(jnp.bfloat16), axis, [(i, i ^ 1) for i in range(4)])
    kept = kept + got.astype(jnp.float32)
    final = lax.dynamic_index_in_dim(kept, high_bit, axis=1, keepdims=False)
    sent = lax.dynamic_index_in_dim(kept, 1 - high_bit, axis=1, keepdims=False)
    got = lax.ppermute(sent.astype(jnp.bfloat16), axis, [(i, i ^ 2) for i in range(4)])
    return (final + got.astype(jnp.float32)).astype(jnp.bfloat16)


def rotate_table(positions, head_width):
    half_width = head_width // 2
    frequency = 10000.0 ** (-(jnp.arange(half_width, dtype=jnp.float32) * 2.0) / head_width)
    angles = positions.astype(jnp.float32)[:, None] * frequency[None, :]
    return (jnp.cos(angles)[:, None, :], jnp.sin(angles)[:, None, :])


def norm_rotate(linear, gain_vec, cosine, sine_table):
    mean_square = jnp.mean(linear * linear, axis=-1, keepdims=True)
    normed = linear * lax.rsqrt(mean_square + norm_eps) * gain_vec
    half_width = linear.shape[-1] // 2
    first_half = normed[..., :half_width]
    second_half = normed[..., half_width:]
    return jnp.concatenate(
        [
            first_half * cosine - second_half * sine_table,
            second_half * cosine + first_half * sine_table,
        ],
        axis=-1,
    )


def block_grad(queries, key_rows, value_rows, cotangent, query_pos, key_pos, windows, score_scale):
    tok_rows, q_heads, head_width = queries.shape
    kv_heads = key_rows.shape[1]
    group_size = q_heads // kv_heads
    query_grp = queries.reshape(tok_rows, kv_heads, group_size, head_width)
    cotan_grp = cotangent.reshape(tok_rows, kv_heads, group_size, head_width)
    scores = score_scale * jnp.einsum(
        "tgjd,sgd->gjts", query_grp, key_rows, preferred_element_type=jnp.float32
    )
    distance = query_pos[:, None] - key_pos[None, :]
    reach = windows.reshape(kv_heads, group_size)[:, :, None, None]
    allowed = (
        (distance[None, None] >= 0)
        & (distance[None, None] < reach)
        & (key_pos >= 0)[None, None, None, :]
    )
    masked = jnp.where(allowed, scores, jnp.float32(-1e30))
    row_peak = jnp.max(masked, axis=-1, keepdims=True)
    row_total = jnp.sum(
        jnp.where(allowed, jnp.exp(masked - row_peak), jnp.float32(0.0)), axis=-1, keepdims=True
    )
    logsum = row_peak + jnp.log(row_total)
    probability = jnp.where(allowed, jnp.exp(masked - logsum), jnp.float32(0.0))
    probs_b = probability.astype(jnp.bfloat16)
    attended = jnp.einsum(
        "gjts,sgd->tgjd", probs_b, value_rows, preferred_element_type=jnp.float32
    ).astype(jnp.bfloat16)
    row_delta = jnp.sum(cotan_grp.astype(jnp.float32) * attended.astype(jnp.float32), axis=-1)
    dprobs = jnp.einsum("tgjd,sgd->gjts", cotan_grp, value_rows, preferred_element_type=jnp.float32)
    dscore = (probability * (dprobs - jnp.transpose(row_delta, (1, 2, 0))[..., None])).astype(
        jnp.bfloat16
    )
    dquery = score_scale * jnp.einsum(
        "gjts,sgd->tgjd", dscore, key_rows, preferred_element_type=jnp.float32
    )
    key_grads = score_scale * jnp.einsum(
        "gjts,tgjd->sgd", dscore, query_grp, preferred_element_type=jnp.float32
    )
    dvalues = jnp.einsum("gjts,tgjd->sgd", probs_b, cotan_grp, preferred_element_type=jnp.float32)
    return (
        attended.reshape(tok_rows, q_heads * head_width),
        dquery.reshape(tok_rows, q_heads, head_width),
        key_grads,
        dvalues,
    )


def body(
    tokens,
    q_weight,
    k_weight,
    v_weight,
    q_gain,
    k_gain,
    windows,
    token_weight,
    loss_mask,
    grad_attn,
):
    tok_rows = tokens.shape[0]
    head_width = q_gain.shape[0]
    q_heads = q_weight.shape[1] // head_width
    kv_heads = k_weight.shape[1] // head_width
    pred_count = WINDOW // tok_rows
    key_span = (pred_count + 1) * tok_rows
    score_scale = QPRE ** (-0.5)
    first_row = lax.axis_index("seq") * tok_rows
    positions = first_row + jnp.arange(tok_rows, dtype=jnp.int32)
    key_pos = first_row - pred_count * tok_rows + jnp.arange(key_span, dtype=jnp.int32)
    kept_weight = token_weight * loss_mask.astype(jnp.float32)
    normalizer = butterfly_sum(jnp.sum(kept_weight), "seq")
    factor = kept_weight * (tok_rows * lax.axis_size("seq") / normalizer)
    cotangent = (
        (grad_attn.astype(jnp.float32) * factor[:, None])
        .astype(jnp.bfloat16)
        .reshape(tok_rows, q_heads, head_width)
    )
    contract = (((1,), (1,)), ((), ()))
    q_cols = q_weight.shape[1]
    k_cols = k_weight.shape[1]
    joined_rows = lax.all_gather(
        jnp.concatenate([q_weight, k_weight, v_weight], axis=1), "seq", axis=0, tiled=True
    )
    all_linear = jnp.dot(tokens, joined_rows, preferred_element_type=jnp.float32)
    q_linear = all_linear[:, :q_cols]
    k_linear = all_linear[:, q_cols : q_cols + k_cols]
    v_linear = all_linear[:, q_cols + k_cols :]
    q_linear = q_linear.reshape(tok_rows, q_heads, head_width)
    k_linear = k_linear.reshape(tok_rows, kv_heads, head_width)
    values = v_linear.astype(jnp.bfloat16)
    cosine, sine_table = rotate_table(positions, head_width)
    q_rot = norm_rotate(q_linear, q_gain, cosine, sine_table).astype(jnp.bfloat16)
    k_rot = norm_rotate(k_linear, k_gain, cosine, sine_table).astype(jnp.bfloat16)
    stacked = jnp.stack([k_rot.reshape(tok_rows, kv_heads * head_width), values])
    received = []
    for offset in range(1, pred_count + 1):
        received.append(passed_along(stacked, "seq", offset))
    extended = jnp.concatenate(received[::-1] + [stacked], axis=1)
    key_rows = extended[0].reshape(key_span, kv_heads, head_width)
    value_rows = extended[1].reshape(key_span, kv_heads, head_width)
    attended, dquery, key_grads, dvalues = block_grad(
        q_rot, key_rows, value_rows, cotangent, positions, key_pos, windows, score_scale
    )
    stacked_grads = jnp.stack(
        [
            key_grads.reshape(key_span, kv_heads * head_width),
            dvalues.reshape(key_span, kv_heads * head_width),
        ]
    )
    local_grads = stacked_grads[:, pred_count * tok_rows :]
    for offset in range(1, pred_count + 1):
        local_grads = local_grads + passed_along(
            stacked_grads[
                :, (pred_count - offset) * tok_rows : (pred_count - offset + 1) * tok_rows
            ].astype(jnp.bfloat16),
            "seq",
            -offset,
        ).astype(jnp.float32)
    key_total = local_grads[0].reshape(tok_rows, kv_heads, head_width)
    _, back_query = jax.vjp(
        lambda linear_in: norm_rotate(linear_in, q_gain, cosine, sine_table), q_linear
    )
    _, back_key = jax.vjp(
        lambda linear_in: norm_rotate(linear_in, k_gain, cosine, sine_table), k_linear
    )
    dq_lin = back_query(dquery)[0].astype(jnp.bfloat16).reshape(tok_rows, q_heads * head_width)
    dk_lin = back_key(key_total)[0].astype(jnp.bfloat16).reshape(tok_rows, kv_heads * head_width)
    dv_lin = local_grads[1].astype(jnp.bfloat16)
    joined_grad = jnp.concatenate([dq_lin, dk_lin, dv_lin], axis=1)
    partial_grad = lax.dot_general(
        joined_grad,
        joined_rows,
        contract,
        preferred_element_type=jnp.float32,
    )
    grad_tokens = head_scatter_sum(partial_grad, "head")
    return (attended, grad_tokens)


def solution(mesh):
    in_specs = (
        P("seq", None),
        P("seq", "head"),
        P("seq", "head"),
        P("seq", "head"),
        P(),
        P(),
        P("head"),
        P("seq"),
        P("seq"),
        P("seq", "head"),
    )
    out_specs = (P("seq", "head"), P("seq", "head"))
    return jax.shard_map(body, mesh=mesh, in_specs=in_specs, out_specs=out_specs, check_vma=False)
```

```python
import jax
import jax.numpy as jnp
from jax import lax
from jax.sharding import PartitionSpec as P

QPRE = 168
WINDOW = 1024


norm_eps = 1e-06


def passed_along(block, axis, distance):
    devices = range(lax.axis_size(axis))
    route = [(i - distance, i) for i in devices if i - distance in devices]
    return lax.ppermute(block, axis, route)


def butterfly_sum(value, axis):
    size = lax.axis_size(axis)
    step = 1
    while step < size:
        value = value + lax.ppermute(value, axis, [(i, i ^ step) for i in range(size)])
        step *= 2
    return value


def head_scatter_sum(partial, axis):
    rows, width = partial.shape
    index = lax.axis_index(axis)
    parts = partial.reshape(rows, 2, 2, width // 4)
    low_bit = index % 2
    high_bit = index // 2
    kept = lax.dynamic_index_in_dim(parts, low_bit, axis=2, keepdims=False)
    sent = lax.dynamic_index_in_dim(parts, 1 - low_bit, axis=2, keepdims=False)
    got = lax.ppermute(sent.astype(jnp.bfloat16), axis, [(i, i ^ 1) for i in range(4)])
    kept = kept + got.astype(jnp.float32)
    final = lax.dynamic_index_in_dim(kept, high_bit, axis=1, keepdims=False)
    sent = lax.dynamic_index_in_dim(kept, 1 - high_bit, axis=1, keepdims=False)
    got = lax.ppermute(sent.astype(jnp.bfloat16), axis, [(i, i ^ 2) for i in range(4)])
    return (final + got.astype(jnp.float32)).astype(jnp.bfloat16)


def rotate_table(positions, head_width):
    half_width = head_width // 2
    frequency = 10000.0 ** (-(jnp.arange(half_width, dtype=jnp.float32) * 2.0) / head_width)
    angles = positions.astype(jnp.float32)[:, None] * frequency[None, :]
    return (jnp.cos(angles)[:, None, :], jnp.sin(angles)[:, None, :])


def norm_rotate(linear, gain_vec, cosine, sine_table):
    mean_square = jnp.mean(linear * linear, axis=-1, keepdims=True)
    normed = linear * lax.rsqrt(mean_square + norm_eps) * gain_vec
    half_width = linear.shape[-1] // 2
    first_half = normed[..., :half_width]
    second_half = normed[..., half_width:]
    return jnp.concatenate(
        [
            first_half * cosine - second_half * sine_table,
            second_half * cosine + first_half * sine_table,
        ],
        axis=-1,
    )


def block_grad(queries, key_rows, value_rows, cotangent, query_pos, key_pos, windows, score_scale):
    tok_rows, q_heads, head_width = queries.shape
    kv_heads = key_rows.shape[1]
    group_size = q_heads // kv_heads
    query_grp = queries.reshape(tok_rows, kv_heads, group_size, head_width)
    cotan_grp = cotangent.reshape(tok_rows, kv_heads, group_size, head_width)
    scores = score_scale * jnp.einsum(
        "tgjd,sgd->gjts", query_grp, key_rows, preferred_element_type=jnp.float32
    )
    distance = query_pos[:, None] - key_pos[None, :]
    reach = windows.reshape(kv_heads, group_size)[:, :, None, None]
    allowed = (
        (distance[None, None] >= 0)
        & (distance[None, None] < reach)
        & (key_pos >= 0)[None, None, None, :]
    )
    masked = jnp.where(allowed, scores, jnp.float32(-1e30))
    row_peak = jnp.max(masked, axis=-1, keepdims=True)
    row_total = jnp.sum(
        jnp.where(allowed, jnp.exp(masked - row_peak), jnp.float32(0.0)), axis=-1, keepdims=True
    )
    logsum = row_peak + jnp.log(row_total)
    probability = jnp.where(allowed, jnp.exp(masked - logsum), jnp.float32(0.0))
    probs_b = probability.astype(jnp.bfloat16)
    attended = jnp.einsum(
        "gjts,sgd->tgjd", probs_b, value_rows, preferred_element_type=jnp.float32
    ).astype(jnp.bfloat16)
    row_delta = jnp.sum(cotan_grp.astype(jnp.float32) * attended.astype(jnp.float32), axis=-1)
    dprobs = jnp.einsum("tgjd,sgd->gjts", cotan_grp, value_rows, preferred_element_type=jnp.float32)
    dscore = (probability * (dprobs - jnp.transpose(row_delta, (1, 2, 0))[..., None])).astype(
        jnp.bfloat16
    )
    dquery = score_scale * jnp.einsum(
        "gjts,sgd->tgjd", dscore, key_rows, preferred_element_type=jnp.float32
    )
    key_grads = score_scale * jnp.einsum(
        "gjts,tgjd->sgd", dscore, query_grp, preferred_element_type=jnp.float32
    )
    dvalues = jnp.einsum("gjts,tgjd->sgd", probs_b, cotan_grp, preferred_element_type=jnp.float32)
    return (
        attended.reshape(tok_rows, q_heads * head_width),
        dquery.reshape(tok_rows, q_heads, head_width),
        key_grads,
        dvalues,
    )


def body(
    tokens,
    q_weight,
    k_weight,
    v_weight,
    q_gain,
    k_gain,
    windows,
    token_weight,
    loss_mask,
    grad_attn,
):
    tok_rows = tokens.shape[0]
    head_width = q_gain.shape[0]
    q_heads = q_weight.shape[1] // head_width
    kv_heads = k_weight.shape[1] // head_width
    pred_count = WINDOW // tok_rows
    key_span = (pred_count + 1) * tok_rows
    score_scale = QPRE ** (-0.5)
    first_row = lax.axis_index("seq") * tok_rows
    positions = first_row + jnp.arange(tok_rows, dtype=jnp.int32)
    key_pos = first_row - pred_count * tok_rows + jnp.arange(key_span, dtype=jnp.int32)
    kept_weight = token_weight * loss_mask.astype(jnp.float32)
    normalizer = butterfly_sum(jnp.sum(kept_weight), "seq")
    factor = kept_weight * (tok_rows * lax.axis_size("seq") / normalizer)
    cotangent = (
        (grad_attn.astype(jnp.float32) * factor[:, None])
        .astype(jnp.bfloat16)
        .reshape(tok_rows, q_heads, head_width)
    )
    contract = (((1,), (1,)), ((), ()))
    q_cols = q_weight.shape[1]
    k_cols = k_weight.shape[1]
    row_block = q_weight.shape[0]
    seq_count = lax.axis_size("seq")
    joined_rows = lax.all_gather(
        jnp.concatenate([q_weight, k_weight, v_weight], axis=1), "seq", axis=0, tiled=False
    )
    token_blocks = tokens.reshape(tok_rows, seq_count, row_block)
    all_linear = jnp.einsum(
        "tsr,src->tc", token_blocks, joined_rows, preferred_element_type=jnp.float32
    )
    q_linear = all_linear[:, :q_cols]
    k_linear = all_linear[:, q_cols : q_cols + k_cols]
    v_linear = all_linear[:, q_cols + k_cols :]
    q_linear = q_linear.reshape(tok_rows, q_heads, head_width)
    k_linear = k_linear.reshape(tok_rows, kv_heads, head_width)
    values = v_linear.astype(jnp.bfloat16)
    cosine, sine_table = rotate_table(positions, head_width)
    q_rot = norm_rotate(q_linear, q_gain, cosine, sine_table).astype(jnp.bfloat16)
    k_rot = norm_rotate(k_linear, k_gain, cosine, sine_table).astype(jnp.bfloat16)
    stacked = jnp.stack([k_rot.reshape(tok_rows, kv_heads * head_width), values])
    received = []
    for offset in range(1, pred_count + 1):
        received.append(passed_along(stacked, "seq", offset))
    extended = jnp.concatenate(received[::-1] + [stacked], axis=1)
    key_rows = extended[0].reshape(key_span, kv_heads, head_width)
    value_rows = extended[1].reshape(key_span, kv_heads, head_width)
    attended, dquery, key_grads, dvalues = block_grad(
        q_rot, key_rows, value_rows, cotangent, positions, key_pos, windows, score_scale
    )
    stacked_grads = jnp.stack(
        [
            key_grads.reshape(key_span, kv_heads * head_width),
            dvalues.reshape(key_span, kv_heads * head_width),
        ]
    )
    local_grads = stacked_grads[:, pred_count * tok_rows :]
    for offset in range(1, pred_count + 1):
        local_grads = local_grads + passed_along(
            stacked_grads[
                :, (pred_count - offset) * tok_rows : (pred_count - offset + 1) * tok_rows
            ].astype(jnp.bfloat16),
            "seq",
            -offset,
        ).astype(jnp.float32)
    key_total = local_grads[0].reshape(tok_rows, kv_heads, head_width)
    _, back_query = jax.vjp(
        lambda linear_in: norm_rotate(linear_in, q_gain, cosine, sine_table), q_linear
    )
    _, back_key = jax.vjp(
        lambda linear_in: norm_rotate(linear_in, k_gain, cosine, sine_table), k_linear
    )
    dq_lin = back_query(dquery)[0].astype(jnp.bfloat16).reshape(tok_rows, q_heads * head_width)
    dk_lin = back_key(key_total)[0].astype(jnp.bfloat16).reshape(tok_rows, kv_heads * head_width)
    dv_lin = local_grads[1].astype(jnp.bfloat16)
    joined_grad = jnp.concatenate([dq_lin, dk_lin, dv_lin], axis=1)
    partial_grad = jnp.einsum(
        "tc,src->tsr", joined_grad, joined_rows, preferred_element_type=jnp.float32
    ).reshape(tok_rows, seq_count * row_block)
    grad_tokens = head_scatter_sum(partial_grad, "head")
    return (attended, grad_tokens)


def solution(mesh):
    in_specs = (
        P("seq", None),
        P("seq", "head"),
        P("seq", "head"),
        P("seq", "head"),
        P(),
        P(),
        P("head"),
        P("seq"),
        P("seq"),
        P("seq", "head"),
    )
    out_specs = (P("seq", "head"), P("seq", "head"))
    return jax.shard_map(body, mesh=mesh, in_specs=in_specs, out_specs=out_specs, check_vma=False)
```

```python
import jax
import jax.numpy as jnp
from jax import lax
from jax.sharding import PartitionSpec as P

QPRE = 168
WINDOW = 1024


norm_eps = 1e-06


def passed_along(block, axis, distance):
    devices = range(lax.axis_size(axis))
    route = [(i - distance, i) for i in devices if i - distance in devices]
    return lax.ppermute(block, axis, route)


def butterfly_sum(value, axis):
    size = lax.axis_size(axis)
    step = 1
    while step < size:
        value = value + lax.ppermute(value, axis, [(i, i ^ step) for i in range(size)])
        step *= 2
    return value


def head_scatter_sum(partial, axis):
    rows, width = partial.shape
    index = lax.axis_index(axis)
    parts = partial.reshape(rows, 2, 2, width // 4)
    low_bit = index % 2
    high_bit = index // 2
    kept = lax.dynamic_index_in_dim(parts, low_bit, axis=2, keepdims=False)
    sent = lax.dynamic_index_in_dim(parts, 1 - low_bit, axis=2, keepdims=False)
    got = lax.ppermute(sent.astype(jnp.bfloat16), axis, [(i, i ^ 1) for i in range(4)])
    kept = kept + got.astype(jnp.float32)
    final = lax.dynamic_index_in_dim(kept, high_bit, axis=1, keepdims=False)
    sent = lax.dynamic_index_in_dim(kept, 1 - high_bit, axis=1, keepdims=False)
    got = lax.ppermute(sent.astype(jnp.bfloat16), axis, [(i, i ^ 2) for i in range(4)])
    return (final + got.astype(jnp.float32)).astype(jnp.bfloat16)


def rotate_table(positions, head_width):
    half_width = head_width // 2
    frequency = 10000.0 ** (-(jnp.arange(half_width, dtype=jnp.float32) * 2.0) / head_width)
    angles = positions.astype(jnp.float32)[:, None] * frequency[None, :]
    return (jnp.cos(angles)[:, None, :], jnp.sin(angles)[:, None, :])


def norm_rotate(linear, gain_vec, cosine, sine_table):
    mean_square = jnp.mean(linear * linear, axis=-1, keepdims=True)
    normed = linear * lax.rsqrt(mean_square + norm_eps) * gain_vec
    half_width = linear.shape[-1] // 2
    first_half = normed[..., :half_width]
    second_half = normed[..., half_width:]
    return jnp.concatenate(
        [
            first_half * cosine - second_half * sine_table,
            second_half * cosine + first_half * sine_table,
        ],
        axis=-1,
    )


def block_grad(queries, key_rows, value_rows, cotangent, query_pos, key_pos, windows, score_scale):
    tok_rows, q_heads, head_width = queries.shape
    kv_heads = key_rows.shape[1]
    group_size = q_heads // kv_heads
    query_grp = queries.reshape(tok_rows, kv_heads, group_size, head_width)
    cotan_grp = cotangent.reshape(tok_rows, kv_heads, group_size, head_width)
    scores = score_scale * jnp.einsum(
        "tgjd,sgd->gjts", query_grp, key_rows, preferred_element_type=jnp.float32
    )
    distance = query_pos[:, None] - key_pos[None, :]
    reach = windows.reshape(kv_heads, group_size)[:, :, None, None]
    allowed = (
        (distance[None, None] >= 0)
        & (distance[None, None] < reach)
        & (key_pos >= 0)[None, None, None, :]
    )
    masked = jnp.where(allowed, scores, jnp.float32(-1e30))
    row_peak = jnp.max(masked, axis=-1, keepdims=True)
    row_total = jnp.sum(
        jnp.where(allowed, jnp.exp(masked - row_peak), jnp.float32(0.0)), axis=-1, keepdims=True
    )
    logsum = row_peak + jnp.log(row_total)
    probability = jnp.where(allowed, jnp.exp(masked - logsum), jnp.float32(0.0))
    probs_b = probability.astype(jnp.bfloat16)
    attended = jnp.einsum(
        "gjts,sgd->tgjd", probs_b, value_rows, preferred_element_type=jnp.float32
    ).astype(jnp.bfloat16)
    row_delta = jnp.sum(cotan_grp.astype(jnp.float32) * attended.astype(jnp.float32), axis=-1)
    dprobs = jnp.einsum("tgjd,sgd->gjts", cotan_grp, value_rows, preferred_element_type=jnp.float32)
    dscore = (probability * (dprobs - jnp.transpose(row_delta, (1, 2, 0))[..., None])).astype(
        jnp.bfloat16
    )
    dquery = score_scale * jnp.einsum(
        "gjts,sgd->tgjd", dscore, key_rows, preferred_element_type=jnp.float32
    )
    key_grads = score_scale * jnp.einsum(
        "gjts,tgjd->sgd", dscore, query_grp, preferred_element_type=jnp.float32
    )
    dvalues = jnp.einsum("gjts,tgjd->sgd", probs_b, cotan_grp, preferred_element_type=jnp.float32)
    return (
        attended.reshape(tok_rows, q_heads * head_width),
        dquery.reshape(tok_rows, q_heads, head_width),
        key_grads,
        dvalues,
    )


def body(
    tokens,
    q_weight,
    k_weight,
    v_weight,
    q_gain,
    k_gain,
    windows,
    token_weight,
    loss_mask,
    grad_attn,
):
    tok_rows = tokens.shape[0]
    head_width = q_gain.shape[0]
    q_heads = q_weight.shape[1] // head_width
    kv_heads = k_weight.shape[1] // head_width
    pred_count = WINDOW // tok_rows
    key_span = (pred_count + 1) * tok_rows
    score_scale = QPRE ** (-0.5)
    first_row = lax.axis_index("seq") * tok_rows
    positions = first_row + jnp.arange(tok_rows, dtype=jnp.int32)
    key_pos = first_row - pred_count * tok_rows + jnp.arange(key_span, dtype=jnp.int32)
    kept_weight = token_weight * loss_mask.astype(jnp.float32)
    normalizer = butterfly_sum(jnp.sum(kept_weight), "seq")
    factor = kept_weight * (tok_rows * lax.axis_size("seq") / normalizer)
    cotangent = (
        (grad_attn.astype(jnp.float32) * factor[:, None])
        .astype(jnp.bfloat16)
        .reshape(tok_rows, q_heads, head_width)
    )
    contract = (((1,), (1,)), ((), ()))
    q_cols = q_weight.shape[1]
    k_cols = k_weight.shape[1]
    row_block = q_weight.shape[0]
    seq_count = lax.axis_size("seq")
    joined_rows = lax.all_gather(
        jnp.concatenate([q_weight, k_weight, v_weight], axis=1), "seq", axis=0, tiled=False
    )
    token_blocks = tokens.reshape(tok_rows, seq_count, row_block)
    all_linear = jnp.einsum(
        "tsr,src->tc", token_blocks, joined_rows, preferred_element_type=jnp.float32
    )
    q_linear = all_linear[:, :q_cols]
    k_linear = all_linear[:, q_cols : q_cols + k_cols]
    v_linear = all_linear[:, q_cols + k_cols :]
    q_linear = q_linear.reshape(tok_rows, q_heads, head_width)
    k_linear = k_linear.reshape(tok_rows, kv_heads, head_width)
    values = v_linear.astype(jnp.bfloat16)
    cosine, sine_table = rotate_table(positions, head_width)
    q_rot = norm_rotate(q_linear, q_gain, cosine, sine_table).astype(jnp.bfloat16)
    k_rot = norm_rotate(k_linear, k_gain, cosine, sine_table).astype(jnp.bfloat16)
    stacked = jnp.stack([k_rot.reshape(tok_rows, kv_heads * head_width), values])
    received = []
    for offset in range(1, pred_count + 1):
        received.append(passed_along(stacked, "seq", offset))
    extended = jnp.concatenate(received[::-1] + [stacked], axis=1)
    key_rows = extended[0].reshape(key_span, kv_heads, head_width)
    value_rows = extended[1].reshape(key_span, kv_heads, head_width)
    attended, dquery, key_grads, dvalues = block_grad(
        q_rot, key_rows, value_rows, cotangent, positions, key_pos, windows, score_scale
    )
    stacked_grads = jnp.stack(
        [
            key_grads.reshape(key_span, kv_heads * head_width),
            dvalues.reshape(key_span, kv_heads * head_width),
        ]
    )
    local_grads = stacked_grads[:, pred_count * tok_rows :]
    for offset in range(1, pred_count + 1):
        local_grads = local_grads + passed_along(
            stacked_grads[
                :, (pred_count - offset) * tok_rows : (pred_count - offset + 1) * tok_rows
            ].astype(jnp.bfloat16),
            "seq",
            -offset,
        ).astype(jnp.float32)
    key_total = local_grads[0].reshape(tok_rows, kv_heads, head_width)
    _, back_query = jax.vjp(
        lambda linear_in: norm_rotate(linear_in, q_gain, cosine, sine_table), q_linear
    )
    _, back_key = jax.vjp(
        lambda linear_in: norm_rotate(linear_in, k_gain, cosine, sine_table), k_linear
    )
    dq_lin = back_query(dquery)[0].astype(jnp.bfloat16).reshape(tok_rows, q_heads * head_width)
    dk_lin = back_key(key_total)[0].astype(jnp.bfloat16).reshape(tok_rows, kv_heads * head_width)
    dv_lin = local_grads[1].astype(jnp.bfloat16)
    joined_grad = jnp.concatenate([dq_lin, dk_lin, dv_lin], axis=1)
    partial_grad = lax.dot_general(
        joined_grad,
        joined_rows.reshape(seq_count * row_block, joined_rows.shape[-1]),
        contract,
        preferred_element_type=jnp.float32,
    )
    grad_tokens = head_scatter_sum(partial_grad, "head")
    return (attended, grad_tokens)


def solution(mesh):
    in_specs = (
        P("seq", None),
        P("seq", "head"),
        P("seq", "head"),
        P("seq", "head"),
        P(),
        P(),
        P("head"),
        P("seq"),
        P("seq"),
        P("seq", "head"),
    )
    out_specs = (P("seq", "head"), P("seq", "head"))
    return jax.shard_map(body, mesh=mesh, in_specs=in_specs, out_specs=out_specs, check_vma=False)
```

```python
import jax
import jax.numpy as jnp
from jax import lax
from jax.sharding import PartitionSpec as P

QPRE = 168
WINDOW = 1024


norm_eps = 1e-06


def passed_along(block, axis, distance):
    devices = range(lax.axis_size(axis))
    route = [(i - distance, i) for i in devices if i - distance in devices]
    return lax.ppermute(block, axis, route)


def butterfly_sum(value, axis):
    size = lax.axis_size(axis)
    step = 1
    while step < size:
        value = value + lax.ppermute(value, axis, [(i, i ^ step) for i in range(size)])
        step *= 2
    return value


def head_scatter_sum(partial, axis):
    rows, width = partial.shape
    index = lax.axis_index(axis)
    parts = partial.reshape(rows, 2, 2, width // 4)
    low_bit = index % 2
    high_bit = index // 2
    kept = lax.dynamic_index_in_dim(parts, low_bit, axis=2, keepdims=False)
    sent = lax.dynamic_index_in_dim(parts, 1 - low_bit, axis=2, keepdims=False)
    got = lax.ppermute(sent.astype(jnp.bfloat16), axis, [(i, i ^ 1) for i in range(4)])
    kept = kept + got.astype(jnp.float32)
    final = lax.dynamic_index_in_dim(kept, high_bit, axis=1, keepdims=False)
    sent = lax.dynamic_index_in_dim(kept, 1 - high_bit, axis=1, keepdims=False)
    got = lax.ppermute(sent.astype(jnp.bfloat16), axis, [(i, i ^ 2) for i in range(4)])
    return (final + got.astype(jnp.float32)).astype(jnp.bfloat16)


def rotate_table(positions, head_width):
    half_width = head_width // 2
    frequency = 10000.0 ** (-(jnp.arange(half_width, dtype=jnp.float32) * 2.0) / head_width)
    angles = positions.astype(jnp.float32)[:, None] * frequency[None, :]
    return (jnp.cos(angles)[:, None, :], jnp.sin(angles)[:, None, :])


def norm_rotate(linear, gain_vec, cosine, sine_table):
    mean_square = jnp.mean(linear * linear, axis=-1, keepdims=True)
    normed = linear * lax.rsqrt(mean_square + norm_eps) * gain_vec
    half_width = linear.shape[-1] // 2
    first_half = normed[..., :half_width]
    second_half = normed[..., half_width:]
    return jnp.concatenate(
        [
            first_half * cosine - second_half * sine_table,
            second_half * cosine + first_half * sine_table,
        ],
        axis=-1,
    )


def block_grad(queries, key_rows, value_rows, cotangent, query_pos, key_pos, windows, score_scale):
    tok_rows, q_heads, head_width = queries.shape
    kv_heads = key_rows.shape[1]
    group_size = q_heads // kv_heads
    query_grp = queries.reshape(tok_rows, kv_heads, group_size, head_width)
    cotan_grp = cotangent.reshape(tok_rows, kv_heads, group_size, head_width)
    scores = score_scale * jnp.einsum(
        "tgjd,sgd->gjts", query_grp, key_rows, preferred_element_type=jnp.float32
    )
    distance = query_pos[:, None] - key_pos[None, :]
    reach = windows.reshape(kv_heads, group_size)[:, :, None, None]
    allowed = (
        (distance[None, None] >= 0)
        & (distance[None, None] < reach)
        & (key_pos >= 0)[None, None, None, :]
    )
    masked = jnp.where(allowed, scores, jnp.float32(-1e30))
    row_peak = jnp.max(masked, axis=-1, keepdims=True)
    row_total = jnp.sum(
        jnp.where(allowed, jnp.exp(masked - row_peak), jnp.float32(0.0)), axis=-1, keepdims=True
    )
    logsum = row_peak + jnp.log(row_total)
    probability = jnp.where(allowed, jnp.exp(masked - logsum), jnp.float32(0.0))
    probs_b = probability.astype(jnp.bfloat16)
    attended = jnp.einsum(
        "gjts,sgd->tgjd", probs_b, value_rows, preferred_element_type=jnp.float32
    ).astype(jnp.bfloat16)
    row_delta = jnp.sum(cotan_grp.astype(jnp.float32) * attended.astype(jnp.float32), axis=-1)
    dprobs = jnp.einsum("tgjd,sgd->gjts", cotan_grp, value_rows, preferred_element_type=jnp.float32)
    dscore = (probability * (dprobs - jnp.transpose(row_delta, (1, 2, 0))[..., None])).astype(
        jnp.bfloat16
    )
    dquery = score_scale * jnp.einsum(
        "gjts,sgd->tgjd", dscore, key_rows, preferred_element_type=jnp.float32
    )
    key_grads = score_scale * jnp.einsum(
        "gjts,tgjd->sgd", dscore, query_grp, preferred_element_type=jnp.float32
    )
    dvalues = jnp.einsum("gjts,tgjd->sgd", probs_b, cotan_grp, preferred_element_type=jnp.float32)
    return (
        attended.reshape(tok_rows, q_heads * head_width),
        dquery.reshape(tok_rows, q_heads, head_width),
        key_grads,
        dvalues,
    )


def body(
    tokens,
    q_weight,
    k_weight,
    v_weight,
    q_gain,
    k_gain,
    windows,
    token_weight,
    loss_mask,
    grad_attn,
):
    tok_rows = tokens.shape[0]
    head_width = q_gain.shape[0]
    q_heads = q_weight.shape[1] // head_width
    kv_heads = k_weight.shape[1] // head_width
    pred_count = WINDOW // tok_rows
    key_span = (pred_count + 1) * tok_rows
    score_scale = QPRE ** (-0.5)
    first_row = lax.axis_index("seq") * tok_rows
    positions = first_row + jnp.arange(tok_rows, dtype=jnp.int32)
    key_pos = first_row - pred_count * tok_rows + jnp.arange(key_span, dtype=jnp.int32)
    kept_weight = token_weight * loss_mask.astype(jnp.float32)
    normalizer = butterfly_sum(jnp.sum(kept_weight), "seq")
    factor = kept_weight * (tok_rows * lax.axis_size("seq") / normalizer)
    cotangent = (
        (grad_attn.astype(jnp.float32) * factor[:, None])
        .astype(jnp.bfloat16)
        .reshape(tok_rows, q_heads, head_width)
    )
    contract = (((1,), (1,)), ((), ()))
    q_cols = q_weight.shape[1]
    k_cols = k_weight.shape[1]
    row_block = q_weight.shape[0]
    seq_count = lax.axis_size("seq")
    joined_rows = lax.all_gather(
        jnp.concatenate([q_weight, k_weight, v_weight], axis=1), "seq", axis=0, tiled=False
    )
    token_blocks = tokens.reshape(tok_rows, seq_count, row_block)
    all_linear = jnp.einsum(
        "tsr,src->tc", token_blocks, joined_rows, preferred_element_type=jnp.float32
    )
    q_linear = all_linear[:, :q_cols]
    k_linear = all_linear[:, q_cols : q_cols + k_cols]
    v_linear = all_linear[:, q_cols + k_cols :]
    q_linear = q_linear.reshape(tok_rows, q_heads, head_width)
    k_linear = k_linear.reshape(tok_rows, kv_heads, head_width)
    values = v_linear.astype(jnp.bfloat16)
    cosine, sine_table = rotate_table(positions, head_width)
    q_rot = norm_rotate(q_linear, q_gain, cosine, sine_table).astype(jnp.bfloat16)
    k_rot = norm_rotate(k_linear, k_gain, cosine, sine_table).astype(jnp.bfloat16)
    stacked = jnp.stack([k_rot.reshape(tok_rows, kv_heads * head_width), values])
    if pred_count == 4:
        near_one = passed_along(stacked, "seq", 1)
        near_two = passed_along(stacked, "seq", 2)
        far_pair = passed_along(jnp.concatenate([near_two, near_one], axis=1), "seq", 2)
        extended = jnp.concatenate([far_pair, near_two, near_one, stacked], axis=1)
    else:
        received = []
        for offset in range(1, pred_count + 1):
            received.append(passed_along(stacked, "seq", offset))
        extended = jnp.concatenate(received[::-1] + [stacked], axis=1)
    key_rows = extended[0].reshape(key_span, kv_heads, head_width)
    value_rows = extended[1].reshape(key_span, kv_heads, head_width)
    attended, dquery, key_grads, dvalues = block_grad(
        q_rot, key_rows, value_rows, cotangent, positions, key_pos, windows, score_scale
    )
    stacked_grads = jnp.stack(
        [
            key_grads.reshape(key_span, kv_heads * head_width),
            dvalues.reshape(key_span, kv_heads * head_width),
        ]
    )
    local_grads = stacked_grads[:, pred_count * tok_rows :]
    if pred_count == 4:
        far_back = passed_along(
            stacked_grads[:, : 2 * tok_rows].astype(jnp.bfloat16), "seq", -2
        ).astype(jnp.float32)
        near_sums = stacked_grads[:, 2 * tok_rows : 4 * tok_rows] + far_back
        local_grads = (
            local_grads
            + passed_along(near_sums[:, :tok_rows].astype(jnp.bfloat16), "seq", -2).astype(
                jnp.float32
            )
            + passed_along(near_sums[:, tok_rows:].astype(jnp.bfloat16), "seq", -1).astype(
                jnp.float32
            )
        )
    else:
        for offset in range(1, pred_count + 1):
            local_grads = local_grads + passed_along(
                stacked_grads[
                    :, (pred_count - offset) * tok_rows : (pred_count - offset + 1) * tok_rows
                ].astype(jnp.bfloat16),
                "seq",
                -offset,
            ).astype(jnp.float32)
    key_total = local_grads[0].reshape(tok_rows, kv_heads, head_width)
    _, back_query = jax.vjp(
        lambda linear_in: norm_rotate(linear_in, q_gain, cosine, sine_table), q_linear
    )
    _, back_key = jax.vjp(
        lambda linear_in: norm_rotate(linear_in, k_gain, cosine, sine_table), k_linear
    )
    dq_lin = back_query(dquery)[0].astype(jnp.bfloat16).reshape(tok_rows, q_heads * head_width)
    dk_lin = back_key(key_total)[0].astype(jnp.bfloat16).reshape(tok_rows, kv_heads * head_width)
    dv_lin = local_grads[1].astype(jnp.bfloat16)
    joined_grad = jnp.concatenate([dq_lin, dk_lin, dv_lin], axis=1)
    partial_grad = lax.dot_general(
        joined_grad,
        joined_rows.reshape(seq_count * row_block, joined_rows.shape[-1]),
        contract,
        preferred_element_type=jnp.float32,
    )
    grad_tokens = head_scatter_sum(partial_grad, "head")
    return (attended, grad_tokens)


def solution(mesh):
    in_specs = (
        P("seq", None),
        P("seq", "head"),
        P("seq", "head"),
        P("seq", "head"),
        P(),
        P(),
        P("head"),
        P("seq"),
        P("seq"),
        P("seq", "head"),
    )
    out_specs = (P("seq", "head"), P("seq", "head"))
    return jax.shard_map(body, mesh=mesh, in_specs=in_specs, out_specs=out_specs, check_vma=False)
```

```python
import jax
import jax.numpy as jnp
from jax import lax
from jax.sharding import PartitionSpec as P

QPRE = 168
WINDOW = 1024


norm_eps = 1e-06


def passed_along(block, axis, distance):
    devices = range(lax.axis_size(axis))
    route = [(i - distance, i) for i in devices if i - distance in devices]
    return lax.ppermute(block, axis, route)


def butterfly_sum(value, axis):
    size = lax.axis_size(axis)
    step = 1
    while step < size:
        value = value + lax.ppermute(value, axis, [(i, i ^ step) for i in range(size)])
        step *= 2
    return value


def head_scatter_sum(partial, axis):
    rows, width = partial.shape
    index = lax.axis_index(axis)
    parts = partial.reshape(rows, 2, 2, width // 4)
    low_bit = index % 2
    high_bit = index // 2
    kept = lax.dynamic_index_in_dim(parts, low_bit, axis=2, keepdims=False)
    sent = lax.dynamic_index_in_dim(parts, 1 - low_bit, axis=2, keepdims=False)
    got = lax.ppermute(sent.astype(jnp.bfloat16), axis, [(i, i ^ 1) for i in range(4)])
    kept = kept + got.astype(jnp.float32)
    final = lax.dynamic_index_in_dim(kept, high_bit, axis=1, keepdims=False)
    sent = lax.dynamic_index_in_dim(kept, 1 - high_bit, axis=1, keepdims=False)
    got = lax.ppermute(sent.astype(jnp.bfloat16), axis, [(i, i ^ 2) for i in range(4)])
    return (final + got.astype(jnp.float32)).astype(jnp.bfloat16)


def rotate_table(positions, head_width):
    half_width = head_width // 2
    frequency = 10000.0 ** (-(jnp.arange(half_width, dtype=jnp.float32) * 2.0) / head_width)
    angles = positions.astype(jnp.float32)[:, None] * frequency[None, :]
    return (jnp.cos(angles)[:, None, :], jnp.sin(angles)[:, None, :])


def norm_rotate(linear, gain_vec, cosine, sine_table):
    mean_square = jnp.mean(linear * linear, axis=-1, keepdims=True)
    normed = linear * lax.rsqrt(mean_square + norm_eps) * gain_vec
    half_width = linear.shape[-1] // 2
    first_half = normed[..., :half_width]
    second_half = normed[..., half_width:]
    return jnp.concatenate(
        [
            first_half * cosine - second_half * sine_table,
            second_half * cosine + first_half * sine_table,
        ],
        axis=-1,
    )


def block_grad(queries, key_rows, value_rows, cotangent, query_pos, key_pos, windows, score_scale):
    tok_rows, q_heads, head_width = queries.shape
    kv_heads = key_rows.shape[1]
    group_size = q_heads // kv_heads
    query_grp = queries.reshape(tok_rows, kv_heads, group_size, head_width)
    cotan_grp = cotangent.reshape(tok_rows, kv_heads, group_size, head_width)
    scores = score_scale * jnp.einsum(
        "tgjd,sgd->gjts", query_grp, key_rows, preferred_element_type=jnp.float32
    )
    distance = query_pos[:, None] - key_pos[None, :]
    reach = windows.reshape(kv_heads, group_size)[:, :, None, None]
    allowed = (
        (distance[None, None] >= 0)
        & (distance[None, None] < reach)
        & (key_pos >= 0)[None, None, None, :]
    )
    masked = jnp.where(allowed, scores, jnp.float32(-1e30))
    row_peak = jnp.max(masked, axis=-1, keepdims=True)
    row_total = jnp.sum(
        jnp.where(allowed, jnp.exp(masked - row_peak), jnp.float32(0.0)), axis=-1, keepdims=True
    )
    logsum = row_peak + jnp.log(row_total)
    probability = jnp.where(allowed, jnp.exp(masked - logsum), jnp.float32(0.0))
    probs_b = probability.astype(jnp.bfloat16)
    attended = jnp.einsum(
        "gjts,sgd->tgjd", probs_b, value_rows, preferred_element_type=jnp.float32
    ).astype(jnp.bfloat16)
    row_delta = jnp.sum(cotan_grp.astype(jnp.float32) * attended.astype(jnp.float32), axis=-1)
    dprobs = jnp.einsum("tgjd,sgd->gjts", cotan_grp, value_rows, preferred_element_type=jnp.float32)
    dscore = (probability * (dprobs - jnp.transpose(row_delta, (1, 2, 0))[..., None])).astype(
        jnp.bfloat16
    )
    dquery = score_scale * jnp.einsum(
        "gjts,sgd->tgjd", dscore, key_rows, preferred_element_type=jnp.float32
    )
    key_grads = score_scale * jnp.einsum(
        "gjts,tgjd->sgd", dscore, query_grp, preferred_element_type=jnp.float32
    )
    dvalues = jnp.einsum("gjts,tgjd->sgd", probs_b, cotan_grp, preferred_element_type=jnp.float32)
    return (
        attended.reshape(tok_rows, q_heads * head_width),
        dquery.reshape(tok_rows, q_heads, head_width),
        key_grads,
        dvalues,
    )


def body(
    tokens,
    q_weight,
    k_weight,
    v_weight,
    q_gain,
    k_gain,
    windows,
    token_weight,
    loss_mask,
    grad_attn,
):
    tok_rows = tokens.shape[0]
    head_width = q_gain.shape[0]
    q_heads = q_weight.shape[1] // head_width
    kv_heads = k_weight.shape[1] // head_width
    pred_count = WINDOW // tok_rows
    key_span = (pred_count + 1) * tok_rows
    score_scale = QPRE ** (-0.5)
    first_row = lax.axis_index("seq") * tok_rows
    positions = first_row + jnp.arange(tok_rows, dtype=jnp.int32)
    key_pos = first_row - pred_count * tok_rows + jnp.arange(key_span, dtype=jnp.int32)
    kept_weight = token_weight * loss_mask.astype(jnp.float32)
    normalizer = butterfly_sum(jnp.sum(kept_weight), "seq")
    factor = kept_weight * (tok_rows * lax.axis_size("seq") / normalizer)
    cotangent = (
        (grad_attn.astype(jnp.float32) * factor[:, None])
        .astype(jnp.bfloat16)
        .reshape(tok_rows, q_heads, head_width)
    )
    contract = (((1,), (1,)), ((), ()))
    q_cols = q_weight.shape[1]
    k_cols = k_weight.shape[1]
    row_block = q_weight.shape[0]
    seq_count = lax.axis_size("seq")
    joined_rows = lax.all_gather(
        jnp.concatenate([q_weight, k_weight, v_weight], axis=1), "seq", axis=0, tiled=False
    )
    token_blocks = tokens.reshape(tok_rows, seq_count, row_block)
    all_linear = jnp.einsum(
        "tsr,src->tc", token_blocks, joined_rows, preferred_element_type=jnp.float32
    )
    q_linear = all_linear[:, :q_cols]
    k_linear = all_linear[:, q_cols : q_cols + k_cols]
    v_linear = all_linear[:, q_cols + k_cols :]
    q_linear = q_linear.reshape(tok_rows, q_heads, head_width)
    k_linear = k_linear.reshape(tok_rows, kv_heads, head_width)
    values = v_linear.astype(jnp.bfloat16)
    cosine, sine_table = rotate_table(positions, head_width)
    q_rot = norm_rotate(q_linear, q_gain, cosine, sine_table).astype(jnp.bfloat16)
    k_rot = norm_rotate(k_linear, k_gain, cosine, sine_table).astype(jnp.bfloat16)
    stacked = jnp.stack([k_rot.reshape(tok_rows, kv_heads * head_width), values])
    if pred_count == 4:
        near_one = passed_along(stacked, "seq", 1)
        near_two = passed_along(stacked, "seq", 2)
        far_pair = passed_along(jnp.concatenate([near_two, near_one], axis=1), "seq", 2)
        extended = jnp.concatenate([far_pair, near_two, near_one, stacked], axis=1)
    else:
        received = []
        for offset in range(1, pred_count + 1):
            received.append(passed_along(stacked, "seq", offset))
        extended = jnp.concatenate(received[::-1] + [stacked], axis=1)
    key_rows = extended[0].reshape(key_span, kv_heads, head_width)
    value_rows = extended[1].reshape(key_span, kv_heads, head_width)
    attended, dquery, key_grads, dvalues = block_grad(
        q_rot, key_rows, value_rows, cotangent, positions, key_pos, windows, score_scale
    )
    stacked_grads = jnp.stack(
        [
            key_grads.reshape(key_span, kv_heads * head_width),
            dvalues.reshape(key_span, kv_heads * head_width),
        ]
    )
    local_grads = stacked_grads[:, pred_count * tok_rows :]
    for offset in range(1, pred_count + 1):
        local_grads = local_grads + passed_along(
            stacked_grads[
                :, (pred_count - offset) * tok_rows : (pred_count - offset + 1) * tok_rows
            ].astype(jnp.bfloat16),
            "seq",
            -offset,
        ).astype(jnp.float32)
    key_total = local_grads[0].reshape(tok_rows, kv_heads, head_width)
    _, back_query = jax.vjp(
        lambda linear_in: norm_rotate(linear_in, q_gain, cosine, sine_table), q_linear
    )
    _, back_key = jax.vjp(
        lambda linear_in: norm_rotate(linear_in, k_gain, cosine, sine_table), k_linear
    )
    dq_lin = back_query(dquery)[0].astype(jnp.bfloat16).reshape(tok_rows, q_heads * head_width)
    dk_lin = back_key(key_total)[0].astype(jnp.bfloat16).reshape(tok_rows, kv_heads * head_width)
    dv_lin = local_grads[1].astype(jnp.bfloat16)
    joined_grad = jnp.concatenate([dq_lin, dk_lin, dv_lin], axis=1)
    partial_grad = lax.dot_general(
        joined_grad,
        joined_rows.reshape(seq_count * row_block, joined_rows.shape[-1]),
        contract,
        preferred_element_type=jnp.float32,
    )
    grad_tokens = head_scatter_sum(partial_grad, "head")
    return (attended, grad_tokens)


def solution(mesh):
    in_specs = (
        P("seq", None),
        P("seq", "head"),
        P("seq", "head"),
        P("seq", "head"),
        P(),
        P(),
        P("head"),
        P("seq"),
        P("seq"),
        P("seq", "head"),
    )
    out_specs = (P("seq", "head"), P("seq", "head"))
    return jax.shard_map(body, mesh=mesh, in_specs=in_specs, out_specs=out_specs, check_vma=False)
```

```python
import jax
import jax.numpy as jnp
from jax import lax
from jax.sharding import PartitionSpec as P

QPRE = 168
WINDOW = 1024


norm_eps = 1e-06


def passed_along(block, axis, distance):
    devices = range(lax.axis_size(axis))
    route = [(i - distance, i) for i in devices if i - distance in devices]
    return lax.ppermute(block, axis, route)


def butterfly_sum(value, axis):
    size = lax.axis_size(axis)
    step = 1
    while step < size:
        value = value + lax.ppermute(value, axis, [(i, i ^ step) for i in range(size)])
        step *= 2
    return value


def head_scatter_sum(partial, axis):
    index = lax.axis_index(axis)
    parts = partial
    low_bit = index % 2
    high_bit = index // 2
    kept = lax.dynamic_index_in_dim(parts, low_bit, axis=2, keepdims=False)
    sent = lax.dynamic_index_in_dim(parts, 1 - low_bit, axis=2, keepdims=False)
    got = lax.ppermute(sent.astype(jnp.bfloat16), axis, [(i, i ^ 1) for i in range(4)])
    kept = kept + got.astype(jnp.float32)
    final = lax.dynamic_index_in_dim(kept, high_bit, axis=1, keepdims=False)
    sent = lax.dynamic_index_in_dim(kept, 1 - high_bit, axis=1, keepdims=False)
    got = lax.ppermute(sent.astype(jnp.bfloat16), axis, [(i, i ^ 2) for i in range(4)])
    return (final + got.astype(jnp.float32)).astype(jnp.bfloat16)


def rotate_table(positions, head_width):
    half_width = head_width // 2
    frequency = 10000.0 ** (-(jnp.arange(half_width, dtype=jnp.float32) * 2.0) / head_width)
    angles = positions.astype(jnp.float32)[:, None] * frequency[None, :]
    return (jnp.cos(angles)[:, None, :], jnp.sin(angles)[:, None, :])


def norm_rotate(linear, gain_vec, cosine, sine_table):
    mean_square = jnp.mean(linear * linear, axis=-1, keepdims=True)
    normed = linear * lax.rsqrt(mean_square + norm_eps) * gain_vec
    half_width = linear.shape[-1] // 2
    first_half = normed[..., :half_width]
    second_half = normed[..., half_width:]
    return jnp.concatenate(
        [
            first_half * cosine - second_half * sine_table,
            second_half * cosine + first_half * sine_table,
        ],
        axis=-1,
    )


def block_grad(queries, key_rows, value_rows, cotangent, query_pos, key_pos, windows, score_scale):
    tok_rows, q_heads, head_width = queries.shape
    kv_heads = key_rows.shape[1]
    group_size = q_heads // kv_heads
    query_grp = queries.reshape(tok_rows, kv_heads, group_size, head_width)
    cotan_grp = cotangent.reshape(tok_rows, kv_heads, group_size, head_width)
    scores = score_scale * jnp.einsum(
        "tgjd,sgd->gjts", query_grp, key_rows, preferred_element_type=jnp.float32
    )
    distance = query_pos[:, None] - key_pos[None, :]
    reach = windows.reshape(kv_heads, group_size)[:, :, None, None]
    allowed = (
        (distance[None, None] >= 0)
        & (distance[None, None] < reach)
        & (key_pos >= 0)[None, None, None, :]
    )
    masked = jnp.where(allowed, scores, jnp.float32(-1e30))
    row_peak = jnp.max(masked, axis=-1, keepdims=True)
    row_total = jnp.sum(
        jnp.where(allowed, jnp.exp(masked - row_peak), jnp.float32(0.0)), axis=-1, keepdims=True
    )
    logsum = row_peak + jnp.log(row_total)
    probability = jnp.where(allowed, jnp.exp(masked - logsum), jnp.float32(0.0))
    probs_b = probability.astype(jnp.bfloat16)
    attended = jnp.einsum(
        "gjts,sgd->tgjd", probs_b, value_rows, preferred_element_type=jnp.float32
    ).astype(jnp.bfloat16)
    row_delta = jnp.sum(cotan_grp.astype(jnp.float32) * attended.astype(jnp.float32), axis=-1)
    dprobs = jnp.einsum("tgjd,sgd->gjts", cotan_grp, value_rows, preferred_element_type=jnp.float32)
    dscore = (probability * (dprobs - jnp.transpose(row_delta, (1, 2, 0))[..., None])).astype(
        jnp.bfloat16
    )
    dquery = score_scale * jnp.einsum(
        "gjts,sgd->tgjd", dscore, key_rows, preferred_element_type=jnp.float32
    )
    key_grads = score_scale * jnp.einsum(
        "gjts,tgjd->sgd", dscore, query_grp, preferred_element_type=jnp.float32
    )
    dvalues = jnp.einsum("gjts,tgjd->sgd", probs_b, cotan_grp, preferred_element_type=jnp.float32)
    return (
        attended.reshape(tok_rows, q_heads * head_width),
        dquery.reshape(tok_rows, q_heads, head_width),
        key_grads,
        dvalues,
    )


def body(
    tokens,
    q_weight,
    k_weight,
    v_weight,
    q_gain,
    k_gain,
    windows,
    token_weight,
    loss_mask,
    grad_attn,
):
    tok_rows = tokens.shape[0]
    head_width = q_gain.shape[0]
    q_heads = q_weight.shape[1] // head_width
    kv_heads = k_weight.shape[1] // head_width
    pred_count = WINDOW // tok_rows
    key_span = (pred_count + 1) * tok_rows
    score_scale = QPRE ** (-0.5)
    first_row = lax.axis_index("seq") * tok_rows
    positions = first_row + jnp.arange(tok_rows, dtype=jnp.int32)
    key_pos = first_row - pred_count * tok_rows + jnp.arange(key_span, dtype=jnp.int32)
    kept_weight = token_weight * loss_mask.astype(jnp.float32)
    normalizer = butterfly_sum(jnp.sum(kept_weight), "seq")
    factor = kept_weight * (tok_rows * lax.axis_size("seq") / normalizer)
    cotangent = (
        (grad_attn.astype(jnp.float32) * factor[:, None])
        .astype(jnp.bfloat16)
        .reshape(tok_rows, q_heads, head_width)
    )
    contract = (((1,), (1,)), ((), ()))
    q_cols = q_weight.shape[1]
    k_cols = k_weight.shape[1]
    row_block = q_weight.shape[0]
    seq_count = lax.axis_size("seq")
    joined_rows = lax.all_gather(
        jnp.concatenate([q_weight, k_weight, v_weight], axis=1), "seq", axis=0, tiled=False
    )
    token_blocks = tokens.reshape(tok_rows, seq_count, row_block)
    kv_linear = jnp.einsum(
        "tsr,src->tc", token_blocks, joined_rows[:, :, q_cols:], preferred_element_type=jnp.float32
    )
    q_linear = jnp.einsum(
        "tsr,src->tc", token_blocks, joined_rows[:, :, :q_cols], preferred_element_type=jnp.float32
    )
    k_linear = kv_linear[:, :k_cols]
    v_linear = kv_linear[:, k_cols:]
    q_linear = q_linear.reshape(tok_rows, q_heads, head_width)
    k_linear = k_linear.reshape(tok_rows, kv_heads, head_width)
    values = v_linear.astype(jnp.bfloat16)
    cosine, sine_table = rotate_table(positions, head_width)
    q_rot = norm_rotate(q_linear, q_gain, cosine, sine_table).astype(jnp.bfloat16)
    k_rot = norm_rotate(k_linear, k_gain, cosine, sine_table).astype(jnp.bfloat16)
    stacked = jnp.stack([k_rot.reshape(tok_rows, kv_heads * head_width), values])
    if pred_count == 4:
        near_one = passed_along(stacked, "seq", 1)
        near_two = passed_along(stacked, "seq", 2)
        far_pair = passed_along(jnp.concatenate([near_two, near_one], axis=1), "seq", 2)
        extended = jnp.concatenate([far_pair, near_two, near_one, stacked], axis=1)
    else:
        received = []
        for offset in range(1, pred_count + 1):
            received.append(passed_along(stacked, "seq", offset))
        extended = jnp.concatenate(received[::-1] + [stacked], axis=1)
    key_rows = extended[0].reshape(key_span, kv_heads, head_width)
    value_rows = extended[1].reshape(key_span, kv_heads, head_width)
    attended, dquery, key_grads, dvalues = block_grad(
        q_rot, key_rows, value_rows, cotangent, positions, key_pos, windows, score_scale
    )
    stacked_grads = jnp.stack(
        [
            key_grads.reshape(key_span, kv_heads * head_width),
            dvalues.reshape(key_span, kv_heads * head_width),
        ]
    )
    local_grads = stacked_grads[:, pred_count * tok_rows :]
    if pred_count == 4:
        far_back = passed_along(
            stacked_grads[:, : 2 * tok_rows].astype(jnp.bfloat16), "seq", -2
        ).astype(jnp.float32)
        near_sums = stacked_grads[:, 2 * tok_rows : 4 * tok_rows] + far_back
        local_grads = (
            local_grads
            + passed_along(near_sums[:, :tok_rows].astype(jnp.bfloat16), "seq", -2).astype(
                jnp.float32
            )
            + passed_along(near_sums[:, tok_rows:].astype(jnp.bfloat16), "seq", -1).astype(
                jnp.float32
            )
        )
    else:
        for offset in range(1, pred_count + 1):
            local_grads = local_grads + passed_along(
                stacked_grads[
                    :, (pred_count - offset) * tok_rows : (pred_count - offset + 1) * tok_rows
                ].astype(jnp.bfloat16),
                "seq",
                -offset,
            ).astype(jnp.float32)
    key_total = local_grads[0].reshape(tok_rows, kv_heads, head_width)
    _, back_query = jax.vjp(
        lambda linear_in: norm_rotate(linear_in, q_gain, cosine, sine_table), q_linear
    )
    _, back_key = jax.vjp(
        lambda linear_in: norm_rotate(linear_in, k_gain, cosine, sine_table), k_linear
    )
    dq_lin = back_query(dquery)[0].astype(jnp.bfloat16).reshape(tok_rows, q_heads * head_width)
    dk_lin = back_key(key_total)[0].astype(jnp.bfloat16).reshape(tok_rows, kv_heads * head_width)
    dv_lin = local_grads[1].astype(jnp.bfloat16)
    flat_rows = joined_rows.reshape(seq_count * row_block, joined_rows.shape[-1])
    query_part = lax.dot_general(
        dq_lin, flat_rows[:, :q_cols], contract, preferred_element_type=jnp.float32
    )
    key_value_part = lax.dot_general(
        jnp.concatenate([dk_lin, dv_lin], axis=1),
        flat_rows[:, q_cols:],
        contract,
        preferred_element_type=jnp.float32,
    )
    quarter_shape = (tok_rows, 2, 2, query_part.shape[1] // 4)
    partial_grad = query_part.reshape(quarter_shape) + key_value_part.reshape(quarter_shape)
    grad_tokens = head_scatter_sum(partial_grad, "head")
    return (attended, grad_tokens)


def solution(mesh):
    in_specs = (
        P("seq", None),
        P("seq", "head"),
        P("seq", "head"),
        P("seq", "head"),
        P(),
        P(),
        P("head"),
        P("seq"),
        P("seq"),
        P("seq", "head"),
    )
    out_specs = (P("seq", "head"), P("seq", "head"))
    return jax.shard_map(body, mesh=mesh, in_specs=in_specs, out_specs=out_specs, check_vma=False)
```

```python
import jax
import jax.numpy as jnp
from jax import lax
from jax.sharding import PartitionSpec as P

QPRE = 168
WINDOW = 1024


norm_eps = 1e-06


def passed_along(block, axis, distance):
    devices = range(lax.axis_size(axis))
    route = [(i - distance, i) for i in devices if i - distance in devices]
    return lax.ppermute(block, axis, route)


def butterfly_sum(value, axis):
    size = lax.axis_size(axis)
    step = 1
    while step < size:
        value = value + lax.ppermute(value, axis, [(i, i ^ step) for i in range(size)])
        step *= 2
    return value


def head_scatter_sum(partial, axis):
    index = lax.axis_index(axis)
    parts = partial
    low_bit = index % 2
    high_bit = index // 2
    kept = lax.dynamic_index_in_dim(parts, low_bit, axis=2, keepdims=False)
    sent = lax.dynamic_index_in_dim(parts, 1 - low_bit, axis=2, keepdims=False)
    got = lax.ppermute(sent.astype(jnp.bfloat16), axis, [(i, i ^ 1) for i in range(4)])
    kept = kept + got.astype(jnp.float32)
    final = lax.dynamic_index_in_dim(kept, high_bit, axis=1, keepdims=False)
    sent = lax.dynamic_index_in_dim(kept, 1 - high_bit, axis=1, keepdims=False)
    got = lax.ppermute(sent.astype(jnp.bfloat16), axis, [(i, i ^ 2) for i in range(4)])
    return (final + got.astype(jnp.float32)).astype(jnp.bfloat16)


def rotate_table(positions, head_width):
    half_width = head_width // 2
    frequency = 10000.0 ** (-(jnp.arange(half_width, dtype=jnp.float32) * 2.0) / head_width)
    angles = positions.astype(jnp.float32)[:, None] * frequency[None, :]
    return (jnp.cos(angles)[:, None, :], jnp.sin(angles)[:, None, :])


def norm_rotate(linear, gain_vec, cosine, sine_table):
    mean_square = jnp.mean(linear * linear, axis=-1, keepdims=True)
    normed = linear * lax.rsqrt(mean_square + norm_eps) * gain_vec
    half_width = linear.shape[-1] // 2
    first_half = normed[..., :half_width]
    second_half = normed[..., half_width:]
    return jnp.concatenate(
        [
            first_half * cosine - second_half * sine_table,
            second_half * cosine + first_half * sine_table,
        ],
        axis=-1,
    )


def block_grad(queries, key_rows, value_rows, cotangent, query_pos, key_pos, windows, score_scale):
    tok_rows, q_heads, head_width = queries.shape
    kv_heads = key_rows.shape[1]
    group_size = q_heads // kv_heads
    query_grp = queries.reshape(tok_rows, kv_heads, group_size, head_width)
    cotan_grp = cotangent.reshape(tok_rows, kv_heads, group_size, head_width)
    scores = score_scale * jnp.einsum(
        "tgjd,sgd->gjts", query_grp, key_rows, preferred_element_type=jnp.float32
    )
    distance = query_pos[:, None] - key_pos[None, :]
    reach = windows.reshape(kv_heads, group_size)[:, :, None, None]
    allowed = (
        (distance[None, None] >= 0)
        & (distance[None, None] < reach)
        & (key_pos >= 0)[None, None, None, :]
    )
    masked = jnp.where(allowed, scores, jnp.float32(-1e30))
    row_peak = jnp.max(masked, axis=-1, keepdims=True)
    row_total = jnp.sum(
        jnp.where(allowed, jnp.exp(masked - row_peak), jnp.float32(0.0)), axis=-1, keepdims=True
    )
    logsum = row_peak + jnp.log(row_total)
    probability = jnp.where(allowed, jnp.exp(masked - logsum), jnp.float32(0.0))
    probs_b = probability.astype(jnp.bfloat16)
    attended = jnp.einsum(
        "gjts,sgd->tgjd", probs_b, value_rows, preferred_element_type=jnp.float32
    ).astype(jnp.bfloat16)
    row_delta = jnp.sum(cotan_grp.astype(jnp.float32) * attended.astype(jnp.float32), axis=-1)
    dprobs = jnp.einsum("tgjd,sgd->gjts", cotan_grp, value_rows, preferred_element_type=jnp.float32)
    dscore = (probability * (dprobs - jnp.transpose(row_delta, (1, 2, 0))[..., None])).astype(
        jnp.bfloat16
    )
    dquery = score_scale * jnp.einsum(
        "gjts,sgd->tgjd", dscore, key_rows, preferred_element_type=jnp.float32
    )
    key_grads = score_scale * jnp.einsum(
        "gjts,tgjd->sgd", dscore, query_grp, preferred_element_type=jnp.float32
    )
    dvalues = jnp.einsum("gjts,tgjd->sgd", probs_b, cotan_grp, preferred_element_type=jnp.float32)
    return (
        attended.reshape(tok_rows, q_heads * head_width),
        dquery.reshape(tok_rows, q_heads, head_width),
        key_grads,
        dvalues,
    )


def body(
    tokens,
    q_weight,
    k_weight,
    v_weight,
    q_gain,
    k_gain,
    windows,
    token_weight,
    loss_mask,
    grad_attn,
):
    tok_rows = tokens.shape[0]
    head_width = q_gain.shape[0]
    q_heads = q_weight.shape[1] // head_width
    kv_heads = k_weight.shape[1] // head_width
    pred_count = WINDOW // tok_rows
    key_span = (pred_count + 1) * tok_rows
    score_scale = QPRE ** (-0.5)
    first_row = lax.axis_index("seq") * tok_rows
    positions = first_row + jnp.arange(tok_rows, dtype=jnp.int32)
    key_pos = first_row - pred_count * tok_rows + jnp.arange(key_span, dtype=jnp.int32)
    kept_weight = token_weight * loss_mask.astype(jnp.float32)
    normalizer = butterfly_sum(jnp.sum(kept_weight), "seq")
    factor = kept_weight * (tok_rows * lax.axis_size("seq") / normalizer)
    cotangent = (
        (grad_attn.astype(jnp.float32) * factor[:, None])
        .astype(jnp.bfloat16)
        .reshape(tok_rows, q_heads, head_width)
    )
    contract = (((1,), (1,)), ((), ()))
    q_cols = q_weight.shape[1]
    k_cols = k_weight.shape[1]
    row_block = q_weight.shape[0]
    seq_count = lax.axis_size("seq")
    joined_rows = lax.all_gather(
        jnp.concatenate([q_weight, k_weight, v_weight], axis=1), "seq", axis=0, tiled=False
    )
    token_blocks = tokens.reshape(tok_rows, seq_count, row_block)
    kv_linear = jnp.einsum(
        "tsr,src->tc", token_blocks, joined_rows[:, :, q_cols:], preferred_element_type=jnp.float32
    )
    q_linear = jnp.einsum(
        "tsr,src->tc", token_blocks, joined_rows[:, :, :q_cols], preferred_element_type=jnp.float32
    )
    k_linear = kv_linear[:, :k_cols]
    v_linear = kv_linear[:, k_cols:]
    q_linear = q_linear.reshape(tok_rows, q_heads, head_width)
    k_linear = k_linear.reshape(tok_rows, kv_heads, head_width)
    values = v_linear.astype(jnp.bfloat16)
    cosine, sine_table = rotate_table(positions, head_width)
    q_rot = norm_rotate(q_linear, q_gain, cosine, sine_table).astype(jnp.bfloat16)
    k_rot = norm_rotate(k_linear, k_gain, cosine, sine_table).astype(jnp.bfloat16)
    stacked = jnp.stack([k_rot.reshape(tok_rows, kv_heads * head_width), values])
    if pred_count == 4:
        near_two = passed_along(stacked, "seq", 2)
        odd_pair = passed_along(jnp.concatenate([near_two, stacked], axis=1), "seq", 1)
        far_one = passed_along(near_two, "seq", 2)
        extended = jnp.concatenate(
            [far_one, odd_pair[:, :tok_rows], near_two, odd_pair[:, tok_rows:], stacked], axis=1
        )
    else:
        received = []
        for offset in range(1, pred_count + 1):
            received.append(passed_along(stacked, "seq", offset))
        extended = jnp.concatenate(received[::-1] + [stacked], axis=1)
    key_rows = extended[0].reshape(key_span, kv_heads, head_width)
    value_rows = extended[1].reshape(key_span, kv_heads, head_width)
    attended, dquery, key_grads, dvalues = block_grad(
        q_rot, key_rows, value_rows, cotangent, positions, key_pos, windows, score_scale
    )
    stacked_grads = jnp.stack(
        [
            key_grads.reshape(key_span, kv_heads * head_width),
            dvalues.reshape(key_span, kv_heads * head_width),
        ]
    )
    local_grads = stacked_grads[:, pred_count * tok_rows :]
    if pred_count == 4:
        odd_back = passed_along(
            jnp.concatenate(
                [stacked_grads[:, tok_rows : 2 * tok_rows], stacked_grads[:, 3 * tok_rows : 4 * tok_rows]],
                axis=1,
            ).astype(jnp.bfloat16),
            "seq",
            -1,
        ).astype(jnp.float32)
        far_back = passed_along(
            stacked_grads[:, :tok_rows].astype(jnp.bfloat16), "seq", -2
        ).astype(jnp.float32)
        middle_sum = stacked_grads[:, 2 * tok_rows : 3 * tok_rows] + odd_back[:, :tok_rows] + far_back
        local_grads = (
            local_grads
            + odd_back[:, tok_rows:]
            + passed_along(middle_sum.astype(jnp.bfloat16), "seq", -2).astype(jnp.float32)
        )
    else:
        for offset in range(1, pred_count + 1):
            local_grads = local_grads + passed_along(
                stacked_grads[
                    :, (pred_count - offset) * tok_rows : (pred_count - offset + 1) * tok_rows
                ].astype(jnp.bfloat16),
                "seq",
                -offset,
            ).astype(jnp.float32)
    key_total = local_grads[0].reshape(tok_rows, kv_heads, head_width)
    _, back_query = jax.vjp(
        lambda linear_in: norm_rotate(linear_in, q_gain, cosine, sine_table), q_linear
    )
    _, back_key = jax.vjp(
        lambda linear_in: norm_rotate(linear_in, k_gain, cosine, sine_table), k_linear
    )
    dq_lin = back_query(dquery)[0].astype(jnp.bfloat16).reshape(tok_rows, q_heads * head_width)
    dk_lin = back_key(key_total)[0].astype(jnp.bfloat16).reshape(tok_rows, kv_heads * head_width)
    dv_lin = local_grads[1].astype(jnp.bfloat16)
    flat_rows = joined_rows.reshape(seq_count * row_block, joined_rows.shape[-1])
    query_part = lax.dot_general(
        dq_lin, flat_rows[:, :q_cols], contract, preferred_element_type=jnp.float32
    )
    key_value_part = lax.dot_general(
        jnp.concatenate([dk_lin, dv_lin], axis=1),
        flat_rows[:, q_cols:],
        contract,
        preferred_element_type=jnp.float32,
    )
    quarter_shape = (tok_rows, 2, 2, query_part.shape[1] // 4)
    partial_grad = query_part.reshape(quarter_shape) + key_value_part.reshape(quarter_shape)
    grad_tokens = head_scatter_sum(partial_grad, "head")
    return (attended, grad_tokens)


def solution(mesh):
    in_specs = (
        P("seq", None),
        P("seq", "head"),
        P("seq", "head"),
        P("seq", "head"),
        P(),
        P(),
        P("head"),
        P("seq"),
        P("seq"),
        P("seq", "head"),
    )
    out_specs = (P("seq", "head"), P("seq", "head"))
    return jax.shard_map(body, mesh=mesh, in_specs=in_specs, out_specs=out_specs, check_vma=False)
```

```python
import jax
import jax.numpy as jnp
from jax import lax
from jax.sharding import PartitionSpec as P

QPRE = 168
WINDOW = 1024


norm_eps = 1e-06


def passed_along(block, axis, distance):
    devices = range(lax.axis_size(axis))
    route = [(i - distance, i) for i in devices if i - distance in devices]
    return lax.ppermute(block, axis, route)


def butterfly_sum(value, axis):
    size = lax.axis_size(axis)
    step = 1
    while step < size:
        value = value + lax.ppermute(value, axis, [(i, i ^ step) for i in range(size)])
        step *= 2
    return value


def head_scatter_sum(partial, axis):
    index = lax.axis_index(axis)
    parts = partial
    low_bit = index % 2
    high_bit = index // 2
    kept = lax.dynamic_index_in_dim(parts, low_bit, axis=2, keepdims=False)
    sent = lax.dynamic_index_in_dim(parts, 1 - low_bit, axis=2, keepdims=False)
    got = lax.ppermute(sent.astype(jnp.bfloat16), axis, [(i, i ^ 1) for i in range(4)])
    kept = kept + got.astype(jnp.float32)
    final = lax.dynamic_index_in_dim(kept, high_bit, axis=1, keepdims=False)
    sent = lax.dynamic_index_in_dim(kept, 1 - high_bit, axis=1, keepdims=False)
    got = lax.ppermute(sent.astype(jnp.bfloat16), axis, [(i, i ^ 2) for i in range(4)])
    return (final + got.astype(jnp.float32)).astype(jnp.bfloat16)


def rotate_table(positions, head_width):
    half_width = head_width // 2
    frequency = 10000.0 ** (-(jnp.arange(half_width, dtype=jnp.float32) * 2.0) / head_width)
    angles = positions.astype(jnp.float32)[:, None] * frequency[None, :]
    return (jnp.cos(angles)[:, None, :], jnp.sin(angles)[:, None, :])


def norm_rotate(linear, gain_vec, cosine, sine_table):
    mean_square = jnp.mean(linear * linear, axis=-1, keepdims=True)
    normed = linear * lax.rsqrt(mean_square + norm_eps) * gain_vec
    half_width = linear.shape[-1] // 2
    first_half = normed[..., :half_width]
    second_half = normed[..., half_width:]
    return jnp.concatenate(
        [
            first_half * cosine - second_half * sine_table,
            second_half * cosine + first_half * sine_table,
        ],
        axis=-1,
    )


def block_grad(queries, key_rows, value_rows, cotangent, query_pos, key_pos, windows, score_scale):
    tok_rows, q_heads, head_width = queries.shape
    kv_heads = key_rows.shape[1]
    group_size = q_heads // kv_heads
    query_grp = queries.reshape(tok_rows, kv_heads, group_size, head_width)
    cotan_grp = cotangent.reshape(tok_rows, kv_heads, group_size, head_width)
    scores = score_scale * jnp.einsum(
        "tgjd,sgd->gjts", query_grp, key_rows, preferred_element_type=jnp.float32
    )
    distance = query_pos[:, None] - key_pos[None, :]
    reach = windows.reshape(kv_heads, group_size)[:, :, None, None]
    allowed = (
        (distance[None, None] >= 0)
        & (distance[None, None] < reach)
        & (key_pos >= 0)[None, None, None, :]
    )
    masked = jnp.where(allowed, scores, jnp.float32(-1e30))
    row_peak = jnp.max(masked, axis=-1, keepdims=True)
    row_total = jnp.sum(
        jnp.where(allowed, jnp.exp(masked - row_peak), jnp.float32(0.0)), axis=-1, keepdims=True
    )
    logsum = row_peak + jnp.log(row_total)
    probability = jnp.where(allowed, jnp.exp(masked - logsum), jnp.float32(0.0))
    probs_b = probability.astype(jnp.bfloat16)
    attended = jnp.einsum(
        "gjts,sgd->tgjd", probs_b, value_rows, preferred_element_type=jnp.float32
    ).astype(jnp.bfloat16)
    row_delta = jnp.sum(cotan_grp.astype(jnp.float32) * attended.astype(jnp.float32), axis=-1)
    dprobs = jnp.einsum("tgjd,sgd->gjts", cotan_grp, value_rows, preferred_element_type=jnp.float32)
    dscore = (probability * (dprobs - jnp.transpose(row_delta, (1, 2, 0))[..., None])).astype(
        jnp.bfloat16
    )
    dquery = score_scale * jnp.einsum(
        "gjts,sgd->tgjd", dscore, key_rows, preferred_element_type=jnp.float32
    )
    key_grads = score_scale * jnp.einsum(
        "gjts,tgjd->sgd", dscore, query_grp, preferred_element_type=jnp.float32
    )
    dvalues = jnp.einsum("gjts,tgjd->sgd", probs_b, cotan_grp, preferred_element_type=jnp.float32)
    return (
        attended.reshape(tok_rows, q_heads * head_width),
        dquery.reshape(tok_rows, q_heads, head_width),
        key_grads,
        dvalues,
    )


def body(
    tokens,
    q_weight,
    k_weight,
    v_weight,
    q_gain,
    k_gain,
    windows,
    token_weight,
    loss_mask,
    grad_attn,
):
    tok_rows = tokens.shape[0]
    head_width = q_gain.shape[0]
    q_heads = q_weight.shape[1] // head_width
    kv_heads = k_weight.shape[1] // head_width
    pred_count = WINDOW // tok_rows
    key_span = (pred_count + 1) * tok_rows
    score_scale = QPRE ** (-0.5)
    first_row = lax.axis_index("seq") * tok_rows
    positions = first_row + jnp.arange(tok_rows, dtype=jnp.int32)
    key_pos = first_row - pred_count * tok_rows + jnp.arange(key_span, dtype=jnp.int32)
    kept_weight = token_weight * loss_mask.astype(jnp.float32)
    normalizer = butterfly_sum(jnp.sum(kept_weight), "seq")
    factor = kept_weight * (tok_rows * lax.axis_size("seq") / normalizer)
    cotangent = (
        (grad_attn.astype(jnp.float32) * factor[:, None])
        .astype(jnp.bfloat16)
        .reshape(tok_rows, q_heads, head_width)
    )
    contract = (((1,), (1,)), ((), ()))
    q_cols = q_weight.shape[1]
    k_cols = k_weight.shape[1]
    row_block = q_weight.shape[0]
    seq_count = lax.axis_size("seq")
    joined_rows = lax.all_gather(
        jnp.concatenate([q_weight, k_weight, v_weight], axis=1), "seq", axis=0, tiled=False
    )
    token_blocks = tokens.reshape(tok_rows, seq_count, row_block)
    kv_linear = jnp.einsum(
        "tsr,src->tc", token_blocks, joined_rows[:, :, q_cols:], preferred_element_type=jnp.float32
    )
    q_linear = jnp.einsum(
        "tsr,src->tc", token_blocks, joined_rows[:, :, :q_cols], preferred_element_type=jnp.float32
    )
    k_linear = kv_linear[:, :k_cols]
    v_linear = kv_linear[:, k_cols:]
    q_linear = q_linear.reshape(tok_rows, q_heads, head_width)
    k_linear = k_linear.reshape(tok_rows, kv_heads, head_width)
    values = v_linear.astype(jnp.bfloat16)
    cosine, sine_table = rotate_table(positions, head_width)
    q_rot = norm_rotate(q_linear, q_gain, cosine, sine_table).astype(jnp.bfloat16)
    k_rot = norm_rotate(k_linear, k_gain, cosine, sine_table).astype(jnp.bfloat16)
    stacked = jnp.stack([k_rot.reshape(tok_rows, kv_heads * head_width), values])
    if pred_count == 4:
        near_two = passed_along(stacked, "seq", 2)
        odd_pair = passed_along(jnp.concatenate([near_two, stacked], axis=1), "seq", 1)
        far_one = passed_along(near_two, "seq", 2)
        extended = jnp.concatenate(
            [far_one, odd_pair[:, :tok_rows], near_two, odd_pair[:, tok_rows:], stacked], axis=1
        )
    else:
        received = []
        for offset in range(1, pred_count + 1):
            received.append(passed_along(stacked, "seq", offset))
        extended = jnp.concatenate(received[::-1] + [stacked], axis=1)
    key_rows = extended[0].reshape(key_span, kv_heads, head_width)
    value_rows = extended[1].reshape(key_span, kv_heads, head_width)
    attended, dquery, key_grads, dvalues = block_grad(
        q_rot, key_rows, value_rows, cotangent, positions, key_pos, windows, score_scale
    )
    stacked_grads = jnp.stack(
        [
            key_grads.reshape(key_span, kv_heads * head_width),
            dvalues.reshape(key_span, kv_heads * head_width),
        ]
    )
    late_rows, stacked_grads = lax.optimization_barrier((joined_rows[:, :, q_cols:], stacked_grads))
    local_grads = stacked_grads[:, pred_count * tok_rows :]
    if pred_count == 4:
        odd_back = passed_along(
            jnp.concatenate(
                [stacked_grads[:, tok_rows : 2 * tok_rows], stacked_grads[:, 3 * tok_rows : 4 * tok_rows]],
                axis=1,
            ).astype(jnp.bfloat16),
            "seq",
            -1,
        ).astype(jnp.float32)
        far_back = passed_along(
            stacked_grads[:, :tok_rows].astype(jnp.bfloat16), "seq", -2
        ).astype(jnp.float32)
        middle_sum = stacked_grads[:, 2 * tok_rows : 3 * tok_rows] + odd_back[:, :tok_rows] + far_back
        local_grads = (
            local_grads
            + odd_back[:, tok_rows:]
            + passed_along(middle_sum.astype(jnp.bfloat16), "seq", -2).astype(jnp.float32)
        )
    else:
        for offset in range(1, pred_count + 1):
            local_grads = local_grads + passed_along(
                stacked_grads[
                    :, (pred_count - offset) * tok_rows : (pred_count - offset + 1) * tok_rows
                ].astype(jnp.bfloat16),
                "seq",
                -offset,
            ).astype(jnp.float32)
    key_total = local_grads[0].reshape(tok_rows, kv_heads, head_width)
    _, back_query = jax.vjp(
        lambda linear_in: norm_rotate(linear_in, q_gain, cosine, sine_table), q_linear
    )
    _, back_key = jax.vjp(
        lambda linear_in: norm_rotate(linear_in, k_gain, cosine, sine_table), k_linear
    )
    dq_lin = back_query(dquery)[0].astype(jnp.bfloat16).reshape(tok_rows, q_heads * head_width)
    dk_lin = back_key(key_total)[0].astype(jnp.bfloat16).reshape(tok_rows, kv_heads * head_width)
    dv_lin = local_grads[1].astype(jnp.bfloat16)
    query_rows = joined_rows[:, :, :q_cols].reshape(seq_count * row_block, q_cols)
    query_part = lax.dot_general(dq_lin, query_rows, contract, preferred_element_type=jnp.float32)
    key_value_part = lax.dot_general(
        jnp.concatenate([dk_lin, dv_lin], axis=1),
        late_rows.reshape(seq_count * row_block, late_rows.shape[-1]),
        contract,
        preferred_element_type=jnp.float32,
    )
    quarter_shape = (tok_rows, 2, 2, query_part.shape[1] // 4)
    partial_grad = query_part.reshape(quarter_shape) + key_value_part.reshape(quarter_shape)
    grad_tokens = head_scatter_sum(partial_grad, "head")
    return (attended, grad_tokens)


def solution(mesh):
    in_specs = (
        P("seq", None),
        P("seq", "head"),
        P("seq", "head"),
        P("seq", "head"),
        P(),
        P(),
        P("head"),
        P("seq"),
        P("seq"),
        P("seq", "head"),
    )
    out_specs = (P("seq", "head"), P("seq", "head"))
    return jax.shard_map(body, mesh=mesh, in_specs=in_specs, out_specs=out_specs, check_vma=False)
```

```python
import jax
import jax.numpy as jnp
from jax import lax
from jax.sharding import PartitionSpec as P

QPRE = 168
WINDOW = 1024


norm_eps = 1e-06


def passed_along(block, axis, distance):
    devices = range(lax.axis_size(axis))
    route = [(i - distance, i) for i in devices if i - distance in devices]
    return lax.ppermute(block, axis, route)


def butterfly_sum(value, axis):
    size = lax.axis_size(axis)
    step = 1
    while step < size:
        value = value + lax.ppermute(value, axis, [(i, i ^ step) for i in range(size)])
        step *= 2
    return value


def head_scatter_sum(partial, axis):
    index = lax.axis_index(axis)
    parts = partial
    low_bit = index % 2
    high_bit = index // 2
    kept = lax.dynamic_index_in_dim(parts, low_bit, axis=2, keepdims=False)
    sent = lax.dynamic_index_in_dim(parts, 1 - low_bit, axis=2, keepdims=False)
    got = lax.ppermute(sent.astype(jnp.bfloat16), axis, [(i, i ^ 1) for i in range(4)])
    kept = kept + got.astype(jnp.float32)
    final = lax.dynamic_index_in_dim(kept, high_bit, axis=1, keepdims=False)
    sent = lax.dynamic_index_in_dim(kept, 1 - high_bit, axis=1, keepdims=False)
    got = lax.ppermute(sent.astype(jnp.bfloat16), axis, [(i, i ^ 2) for i in range(4)])
    return (final + got.astype(jnp.float32)).astype(jnp.bfloat16)


def rotate_table(positions, head_width):
    half_width = head_width // 2
    frequency = 10000.0 ** (-(jnp.arange(half_width, dtype=jnp.float32) * 2.0) / head_width)
    angles = positions.astype(jnp.float32)[:, None] * frequency[None, :]
    return (jnp.cos(angles)[:, None, :], jnp.sin(angles)[:, None, :])


def norm_rotate(linear, gain_vec, cosine, sine_table):
    mean_square = jnp.mean(linear * linear, axis=-1, keepdims=True)
    normed = linear * lax.rsqrt(mean_square + norm_eps) * gain_vec
    half_width = linear.shape[-1] // 2
    first_half = normed[..., :half_width]
    second_half = normed[..., half_width:]
    return jnp.concatenate(
        [
            first_half * cosine - second_half * sine_table,
            second_half * cosine + first_half * sine_table,
        ],
        axis=-1,
    )


def block_grad(queries, key_rows, value_rows, cotangent, query_pos, key_pos, windows, score_scale):
    tok_rows, q_heads, head_width = queries.shape
    kv_heads = key_rows.shape[1]
    group_size = q_heads // kv_heads
    query_grp = queries.reshape(tok_rows, kv_heads, group_size, head_width)
    cotan_grp = cotangent.reshape(tok_rows, kv_heads, group_size, head_width)
    scores = score_scale * jnp.einsum(
        "tgjd,sgd->gjts", query_grp, key_rows, preferred_element_type=jnp.float32
    )
    distance = query_pos[:, None] - key_pos[None, :]
    reach = windows.reshape(kv_heads, group_size)[:, :, None, None]
    allowed = (
        (distance[None, None] >= 0)
        & (distance[None, None] < reach)
        & (key_pos >= 0)[None, None, None, :]
    )
    masked = jnp.where(allowed, scores, jnp.float32(-1e30))
    row_peak = jnp.max(masked, axis=-1, keepdims=True)
    row_total = jnp.sum(
        jnp.where(allowed, jnp.exp(masked - row_peak), jnp.float32(0.0)), axis=-1, keepdims=True
    )
    logsum = row_peak + jnp.log(row_total)
    probability = jnp.where(allowed, jnp.exp(masked - logsum), jnp.float32(0.0))
    probs_b = probability.astype(jnp.bfloat16)
    attended = jnp.einsum(
        "gjts,sgd->tgjd", probs_b, value_rows, preferred_element_type=jnp.float32
    ).astype(jnp.bfloat16)
    row_delta = jnp.sum(cotan_grp.astype(jnp.float32) * attended.astype(jnp.float32), axis=-1)
    dprobs = jnp.einsum("tgjd,sgd->gjts", cotan_grp, value_rows, preferred_element_type=jnp.float32)
    dscore = (probability * (dprobs - jnp.transpose(row_delta, (1, 2, 0))[..., None])).astype(
        jnp.bfloat16
    )
    dquery = score_scale * jnp.einsum(
        "gjts,sgd->tgjd", dscore, key_rows, preferred_element_type=jnp.float32
    )
    key_grads = score_scale * jnp.einsum(
        "gjts,tgjd->sgd", dscore, query_grp, preferred_element_type=jnp.float32
    )
    dvalues = jnp.einsum("gjts,tgjd->sgd", probs_b, cotan_grp, preferred_element_type=jnp.float32)
    return (
        attended.reshape(tok_rows, q_heads * head_width),
        dquery.reshape(tok_rows, q_heads, head_width),
        key_grads,
        dvalues,
    )


def body(
    tokens,
    q_weight,
    k_weight,
    v_weight,
    q_gain,
    k_gain,
    windows,
    token_weight,
    loss_mask,
    grad_attn,
):
    tok_rows = tokens.shape[0]
    head_width = q_gain.shape[0]
    q_heads = q_weight.shape[1] // head_width
    kv_heads = k_weight.shape[1] // head_width
    pred_count = WINDOW // tok_rows
    key_span = (pred_count + 1) * tok_rows
    score_scale = QPRE ** (-0.5)
    first_row = lax.axis_index("seq") * tok_rows
    positions = first_row + jnp.arange(tok_rows, dtype=jnp.int32)
    key_pos = first_row - pred_count * tok_rows + jnp.arange(key_span, dtype=jnp.int32)
    kept_weight = token_weight * loss_mask.astype(jnp.float32)
    normalizer = butterfly_sum(jnp.sum(kept_weight), "seq")
    factor = kept_weight * (tok_rows * lax.axis_size("seq") / normalizer)
    cotangent = (
        (grad_attn.astype(jnp.float32) * factor[:, None])
        .astype(jnp.bfloat16)
        .reshape(tok_rows, q_heads, head_width)
    )
    contract = (((1,), (1,)), ((), ()))
    q_cols = q_weight.shape[1]
    k_cols = k_weight.shape[1]
    row_block = q_weight.shape[0]
    seq_count = lax.axis_size("seq")
    joined_rows = lax.all_gather(
        jnp.concatenate([q_weight, k_weight, v_weight], axis=1), "seq", axis=0, tiled=False
    )
    token_blocks = tokens.reshape(tok_rows, seq_count, row_block)
    kv_linear = jnp.einsum(
        "tsr,src->tc", token_blocks, joined_rows[:, :, q_cols:], preferred_element_type=jnp.float32
    )
    q_linear = jnp.einsum(
        "tsr,src->tc", token_blocks, joined_rows[:, :, :q_cols], preferred_element_type=jnp.float32
    )
    k_linear = kv_linear[:, :k_cols]
    v_linear = kv_linear[:, k_cols:]
    q_linear = q_linear.reshape(tok_rows, q_heads, head_width)
    k_linear = k_linear.reshape(tok_rows, kv_heads, head_width)
    values = v_linear.astype(jnp.bfloat16)
    cosine, sine_table = rotate_table(positions, head_width)
    q_rot = norm_rotate(q_linear, q_gain, cosine, sine_table).astype(jnp.bfloat16)
    k_rot = norm_rotate(k_linear, k_gain, cosine, sine_table).astype(jnp.bfloat16)
    stacked = jnp.stack([k_rot.reshape(tok_rows, kv_heads * head_width), values])
    if pred_count == 4:
        near_two = passed_along(stacked, "seq", 2)
        odd_pair = passed_along(jnp.concatenate([near_two, stacked], axis=1), "seq", 1)
        far_one = passed_along(near_two, "seq", 2)
        extended = jnp.concatenate(
            [far_one, odd_pair[:, :tok_rows], near_two, odd_pair[:, tok_rows:], stacked], axis=1
        )
    else:
        received = []
        for offset in range(1, pred_count + 1):
            received.append(passed_along(stacked, "seq", offset))
        extended = jnp.concatenate(received[::-1] + [stacked], axis=1)
    key_rows = extended[0].reshape(key_span, kv_heads, head_width)
    value_rows = extended[1].reshape(key_span, kv_heads, head_width)
    attended, dquery, key_grads, dvalues = block_grad(
        q_rot, key_rows, value_rows, cotangent, positions, key_pos, windows, score_scale
    )
    stacked_grads = jnp.stack(
        [
            key_grads.reshape(key_span, kv_heads * head_width),
            dvalues.reshape(key_span, kv_heads * head_width),
        ]
    )
    local_grads = stacked_grads[:, pred_count * tok_rows :]
    if pred_count == 4:
        odd_back = passed_along(
            jnp.concatenate(
                [stacked_grads[:, tok_rows : 2 * tok_rows], stacked_grads[:, 3 * tok_rows : 4 * tok_rows]],
                axis=1,
            ).astype(jnp.bfloat16),
            "seq",
            -1,
        ).astype(jnp.float32)
        far_back = passed_along(
            stacked_grads[:, :tok_rows].astype(jnp.bfloat16), "seq", -2
        ).astype(jnp.float32)
        middle_sum = stacked_grads[:, 2 * tok_rows : 3 * tok_rows] + odd_back[:, :tok_rows] + far_back
        local_grads = (
            local_grads
            + odd_back[:, tok_rows:]
            + passed_along(middle_sum.astype(jnp.bfloat16), "seq", -2).astype(jnp.float32)
        )
    else:
        for offset in range(1, pred_count + 1):
            local_grads = local_grads + passed_along(
                stacked_grads[
                    :, (pred_count - offset) * tok_rows : (pred_count - offset + 1) * tok_rows
                ].astype(jnp.bfloat16),
                "seq",
                -offset,
            ).astype(jnp.float32)
    key_total = local_grads[0].reshape(tok_rows, kv_heads, head_width)
    _, back_query = jax.vjp(
        lambda linear_in: norm_rotate(linear_in, q_gain, cosine, sine_table), q_linear
    )
    _, back_key = jax.vjp(
        lambda linear_in: norm_rotate(linear_in, k_gain, cosine, sine_table), k_linear
    )
    dq_lin = back_query(dquery)[0].astype(jnp.bfloat16).reshape(tok_rows, q_heads * head_width)
    dk_lin = back_key(key_total)[0].astype(jnp.bfloat16).reshape(tok_rows, kv_heads * head_width)
    dv_lin = local_grads[1].astype(jnp.bfloat16)
    flat_rows = joined_rows.reshape(seq_count * row_block, joined_rows.shape[-1])
    query_part = lax.dot_general(
        dq_lin, flat_rows[:, :q_cols], contract, preferred_element_type=jnp.float32
    )
    key_value_part = lax.dot_general(
        jnp.concatenate([dk_lin, dv_lin], axis=1),
        flat_rows[:, q_cols:],
        contract,
        preferred_element_type=jnp.float32,
    )
    quarter_shape = (tok_rows, 2, 2, query_part.shape[1] // 4)
    partial_grad = query_part.reshape(quarter_shape) + key_value_part.reshape(quarter_shape)
    half_rows = tok_rows // 2
    grad_tokens = jnp.concatenate(
        [
            head_scatter_sum(partial_grad[:half_rows], "head"),
            head_scatter_sum(partial_grad[half_rows:], "head"),
        ],
        axis=0,
    )
    return (attended, grad_tokens)


def solution(mesh):
    in_specs = (
        P("seq", None),
        P("seq", "head"),
        P("seq", "head"),
        P("seq", "head"),
        P(),
        P(),
        P("head"),
        P("seq"),
        P("seq"),
        P("seq", "head"),
    )
    out_specs = (P("seq", "head"), P("seq", "head"))
    return jax.shard_map(body, mesh=mesh, in_specs=in_specs, out_specs=out_specs, check_vma=False)
```

```python
import jax
import jax.numpy as jnp
from jax import lax
from jax.sharding import PartitionSpec as P

QPRE = 168
WINDOW = 1024


norm_eps = 1e-06


def passed_along(block, axis, distance):
    devices = range(lax.axis_size(axis))
    route = [(i - distance, i) for i in devices if i - distance in devices]
    return lax.ppermute(block, axis, route)


def butterfly_sum(value, axis):
    size = lax.axis_size(axis)
    step = 1
    while step < size:
        value = value + lax.ppermute(value, axis, [(i, i ^ step) for i in range(size)])
        step *= 2
    return value


def head_scatter_sum(partial, axis):
    index = lax.axis_index(axis)
    parts = partial
    low_bit = index % 2
    high_bit = index // 2
    kept = lax.dynamic_index_in_dim(parts, low_bit, axis=2, keepdims=False)
    sent = lax.dynamic_index_in_dim(parts, 1 - low_bit, axis=2, keepdims=False)
    got = lax.ppermute(sent.astype(jnp.bfloat16), axis, [(i, i ^ 1) for i in range(4)])
    kept = kept + got.astype(jnp.float32)
    final = lax.dynamic_index_in_dim(kept, high_bit, axis=1, keepdims=False)
    sent = lax.dynamic_index_in_dim(kept, 1 - high_bit, axis=1, keepdims=False)
    got = lax.ppermute(sent.astype(jnp.bfloat16), axis, [(i, i ^ 2) for i in range(4)])
    return (final + got.astype(jnp.float32)).astype(jnp.bfloat16)


def rotate_table(positions, head_width):
    half_width = head_width // 2
    frequency = 10000.0 ** (-(jnp.arange(half_width, dtype=jnp.float32) * 2.0) / head_width)
    angles = positions.astype(jnp.float32)[:, None] * frequency[None, :]
    return (jnp.cos(angles)[:, None, :], jnp.sin(angles)[:, None, :])


def norm_rotate(linear, gain_vec, cosine, sine_table):
    mean_square = jnp.mean(linear * linear, axis=-1, keepdims=True)
    normed = linear * lax.rsqrt(mean_square + norm_eps) * gain_vec
    half_width = linear.shape[-1] // 2
    first_half = normed[..., :half_width]
    second_half = normed[..., half_width:]
    return jnp.concatenate(
        [
            first_half * cosine - second_half * sine_table,
            second_half * cosine + first_half * sine_table,
        ],
        axis=-1,
    )


def block_grad(queries, key_rows, value_rows, cotangent, query_pos, key_pos, windows, score_scale):
    tok_rows, q_heads, head_width = queries.shape
    kv_heads = key_rows.shape[1]
    group_size = q_heads // kv_heads
    query_grp = queries.reshape(tok_rows, kv_heads, group_size, head_width)
    cotan_grp = cotangent.reshape(tok_rows, kv_heads, group_size, head_width)
    scores = score_scale * jnp.einsum(
        "tgjd,sgd->gjts", query_grp, key_rows, preferred_element_type=jnp.float32
    )
    distance = query_pos[:, None] - key_pos[None, :]
    reach = windows.reshape(kv_heads, group_size)[:, :, None, None]
    allowed = (
        (distance[None, None] >= 0)
        & (distance[None, None] < reach)
        & (key_pos >= 0)[None, None, None, :]
    )
    masked = jnp.where(allowed, scores, jnp.float32(-1e30))
    row_peak = jnp.max(masked, axis=-1, keepdims=True)
    row_total = jnp.sum(
        jnp.where(allowed, jnp.exp(masked - row_peak), jnp.float32(0.0)), axis=-1, keepdims=True
    )
    logsum = row_peak + jnp.log(row_total)
    probability = jnp.where(allowed, jnp.exp(masked - logsum), jnp.float32(0.0))
    probs_b = probability.astype(jnp.bfloat16)
    attended = jnp.einsum(
        "gjts,sgd->tgjd", probs_b, value_rows, preferred_element_type=jnp.float32
    ).astype(jnp.bfloat16)
    row_delta = jnp.sum(cotan_grp.astype(jnp.float32) * attended.astype(jnp.float32), axis=-1)
    dprobs = jnp.einsum("tgjd,sgd->gjts", cotan_grp, value_rows, preferred_element_type=jnp.float32)
    dscore = (probability * (dprobs - jnp.transpose(row_delta, (1, 2, 0))[..., None])).astype(
        jnp.bfloat16
    )
    dquery = score_scale * jnp.einsum(
        "gjts,sgd->tgjd", dscore, key_rows, preferred_element_type=jnp.float32
    )
    key_grads = score_scale * jnp.einsum(
        "gjts,tgjd->sgd", dscore, query_grp, preferred_element_type=jnp.float32
    )
    dvalues = jnp.einsum("gjts,tgjd->sgd", probs_b, cotan_grp, preferred_element_type=jnp.float32)
    return (
        attended.reshape(tok_rows, q_heads * head_width),
        dquery.reshape(tok_rows, q_heads, head_width),
        key_grads,
        dvalues,
    )


def body(
    tokens,
    q_weight,
    k_weight,
    v_weight,
    q_gain,
    k_gain,
    windows,
    token_weight,
    loss_mask,
    grad_attn,
):
    tok_rows = tokens.shape[0]
    head_width = q_gain.shape[0]
    q_heads = q_weight.shape[1] // head_width
    kv_heads = k_weight.shape[1] // head_width
    pred_count = WINDOW // tok_rows
    key_span = (pred_count + 1) * tok_rows
    score_scale = QPRE ** (-0.5)
    first_row = lax.axis_index("seq") * tok_rows
    positions = first_row + jnp.arange(tok_rows, dtype=jnp.int32)
    key_pos = first_row - pred_count * tok_rows + jnp.arange(key_span, dtype=jnp.int32)
    kept_weight = token_weight * loss_mask.astype(jnp.float32)
    normalizer = butterfly_sum(jnp.sum(kept_weight), "seq")
    factor = kept_weight * (tok_rows * lax.axis_size("seq") / normalizer)
    cotangent = (
        (grad_attn.astype(jnp.float32) * factor[:, None])
        .astype(jnp.bfloat16)
        .reshape(tok_rows, q_heads, head_width)
    )
    contract = (((1,), (1,)), ((), ()))
    q_cols = q_weight.shape[1]
    k_cols = k_weight.shape[1]
    row_block = q_weight.shape[0]
    seq_count = lax.axis_size("seq")
    joined_rows = lax.all_gather(
        jnp.concatenate([q_weight, k_weight, v_weight], axis=1), "seq", axis=0, tiled=False
    )
    token_blocks = tokens.reshape(tok_rows, seq_count, row_block)
    kv_linear = jnp.einsum(
        "tsr,src->tc", token_blocks, joined_rows[:, :, q_cols:], preferred_element_type=jnp.float32
    )
    q_linear = jnp.einsum(
        "tsr,src->tc", token_blocks, joined_rows[:, :, :q_cols], preferred_element_type=jnp.float32
    )
    k_linear = kv_linear[:, :k_cols]
    v_linear = kv_linear[:, k_cols:]
    q_linear = q_linear.reshape(tok_rows, q_heads, head_width)
    k_linear = k_linear.reshape(tok_rows, kv_heads, head_width)
    values = v_linear.astype(jnp.bfloat16)
    cosine, sine_table = rotate_table(positions, head_width)
    q_rot = norm_rotate(q_linear, q_gain, cosine, sine_table).astype(jnp.bfloat16)
    k_rot = norm_rotate(k_linear, k_gain, cosine, sine_table).astype(jnp.bfloat16)
    stacked = jnp.stack([k_rot.reshape(tok_rows, kv_heads * head_width), values])
    if pred_count == 4:
        near_one = passed_along(stacked, "seq", 1)
        near_two = passed_along(stacked, "seq", 2)
        near_three = passed_along(near_two, "seq", 1)
        far_one = passed_along(near_two, "seq", 2)
        extended = jnp.concatenate([far_one, near_three, near_two, near_one, stacked], axis=1)
    else:
        received = []
        for offset in range(1, pred_count + 1):
            received.append(passed_along(stacked, "seq", offset))
        extended = jnp.concatenate(received[::-1] + [stacked], axis=1)
    key_rows = extended[0].reshape(key_span, kv_heads, head_width)
    value_rows = extended[1].reshape(key_span, kv_heads, head_width)
    attended, dquery, key_grads, dvalues = block_grad(
        q_rot, key_rows, value_rows, cotangent, positions, key_pos, windows, score_scale
    )
    stacked_grads = jnp.stack(
        [
            key_grads.reshape(key_span, kv_heads * head_width),
            dvalues.reshape(key_span, kv_heads * head_width),
        ]
    )
    local_grads = stacked_grads[:, pred_count * tok_rows :]
    if pred_count == 4:
        odd_back = passed_along(
            jnp.concatenate(
                [stacked_grads[:, tok_rows : 2 * tok_rows], stacked_grads[:, 3 * tok_rows : 4 * tok_rows]],
                axis=1,
            ).astype(jnp.bfloat16),
            "seq",
            -1,
        ).astype(jnp.float32)
        far_back = passed_along(
            stacked_grads[:, :tok_rows].astype(jnp.bfloat16), "seq", -2
        ).astype(jnp.float32)
        middle_sum = stacked_grads[:, 2 * tok_rows : 3 * tok_rows] + odd_back[:, :tok_rows] + far_back
        local_grads = (
            local_grads
            + odd_back[:, tok_rows:]
            + passed_along(middle_sum.astype(jnp.bfloat16), "seq", -2).astype(jnp.float32)
        )
    else:
        for offset in range(1, pred_count + 1):
            local_grads = local_grads + passed_along(
                stacked_grads[
                    :, (pred_count - offset) * tok_rows : (pred_count - offset + 1) * tok_rows
                ].astype(jnp.bfloat16),
                "seq",
                -offset,
            ).astype(jnp.float32)
    key_total = local_grads[0].reshape(tok_rows, kv_heads, head_width)
    _, back_query = jax.vjp(
        lambda linear_in: norm_rotate(linear_in, q_gain, cosine, sine_table), q_linear
    )
    _, back_key = jax.vjp(
        lambda linear_in: norm_rotate(linear_in, k_gain, cosine, sine_table), k_linear
    )
    dq_lin = back_query(dquery)[0].astype(jnp.bfloat16).reshape(tok_rows, q_heads * head_width)
    dk_lin = back_key(key_total)[0].astype(jnp.bfloat16).reshape(tok_rows, kv_heads * head_width)
    dv_lin = local_grads[1].astype(jnp.bfloat16)
    flat_rows = joined_rows.reshape(seq_count * row_block, joined_rows.shape[-1])
    query_part = lax.dot_general(
        dq_lin, flat_rows[:, :q_cols], contract, preferred_element_type=jnp.float32
    )
    key_value_part = lax.dot_general(
        jnp.concatenate([dk_lin, dv_lin], axis=1),
        flat_rows[:, q_cols:],
        contract,
        preferred_element_type=jnp.float32,
    )
    quarter_shape = (tok_rows, 2, 2, query_part.shape[1] // 4)
    partial_grad = query_part.reshape(quarter_shape) + key_value_part.reshape(quarter_shape)
    half_rows = tok_rows // 2
    grad_tokens = jnp.concatenate(
        [
            head_scatter_sum(partial_grad[:half_rows], "head"),
            head_scatter_sum(partial_grad[half_rows:], "head"),
        ],
        axis=0,
    )
    return (attended, grad_tokens)


def solution(mesh):
    in_specs = (
        P("seq", None),
        P("seq", "head"),
        P("seq", "head"),
        P("seq", "head"),
        P(),
        P(),
        P("head"),
        P("seq"),
        P("seq"),
        P("seq", "head"),
    )
    out_specs = (P("seq", "head"), P("seq", "head"))
    return jax.shard_map(body, mesh=mesh, in_specs=in_specs, out_specs=out_specs, check_vma=False)
```
